32 devices in a mesh: pipe: 2 (over core), dp: 8 (over z, x), tensor: 2 (over y).
Axes of the slice: x: 2, y: 2, z: 4, core: 2. Of those that a mesh axis runs over, the one named last changes fastest.
Arguments:
- normed_input: bfloat16 [2, 8, 1024, 4096], P('pipe', None, 'dp')
- key_grad: bfloat16 [2, 8, 1024, 512], P('pipe', None, 'dp', 'tensor')
- live_slots: int32 [2, 8], P('pipe'), may hold values from 0 to 1, as said below
- master: float32 [2, 4096, 512], P('pipe', 'dp', 'tensor'), may hold values from -4 to 4
- first_moment: float32 [2, 4096, 512], P('pipe', 'dp', 'tensor'), may hold values from -0.0009765625 to 0.0009765625
- second_moment: float32 [2, 4096, 512], P('pipe', 'dp', 'tensor'), as said below
Outputs:
- update: bfloat16 [2, 4096, 512], P('pipe', None, 'tensor')
The draws below stay inside these ranges and needn't reach their ends.
Inputs may be any that keep to these rules, and one draw needn't show every extreme that they name: `live_slots`: in every draw exactly one section has all 8 slots live; every other section has at least one live and at least one dead slot. `second_moment`: every entry is positive.
All inputs are finite; a program needn't handle non-finite values.
Results may differ from the reference program's by a relative error of at most 0.0004.
Values may be sent and summed in bfloat16 or wider, within the bound.
No kernel may reach another device: no remote copies, remote signals or barrier semaphores. Data moves between devices by JAX's collectives and lax.ppermute only.
A program may use at most 64 MiB of HBM per device.

```python
import math
import jax
import jax.numpy as jnp
from jax import lax

FEAT = 4096
MB = 8
TOK_MB = 128
SECTIONS = 2
KC = 512
TOK_ROWS = 1024
PARAMS = 4194304


def spread_scale(key, full_shape):
    return jnp.exp(jax.random.uniform(key, full_shape, jnp.float32, 0.0, math.log(10.0))) / math.sqrt(10.0)


def input_values(key):
    key_list = jax.random.split(jax.random.fold_in(key, 101), 5)
    full_shape = (SECTIONS, MB, TOK_ROWS, FEAT)
    position = jnp.arange(FEAT, dtype=jnp.float32) / FEAT
    values = jax.random.normal(key_list[0], full_shape, jnp.float32)
    rising = 3.0 ** (0.5 * position)
    row_scale = spread_scale(key_list[1], (SECTIONS, MB, TOK_ROWS, 1))
    column_scale = spread_scale(key_list[2], (FEAT,)) * rising
    groups = TOK_ROWS // TOK_MB
    pairing = jax.random.permutation(key_list[4], groups)
    token_group = jnp.arange(TOK_ROWS) // TOK_MB
    column_group = jnp.arange(FEAT) // (FEAT // groups)
    spike = jnp.where(pairing[token_group][:, None] == column_group[None, :], 6.0, 1.0)
    return values * row_scale * column_scale * spike


def draw_normed_input(key, part):
    return input_values(key).astype(jnp.bfloat16)


def draw_key_grad(key, part):
    inputs = input_values(key)
    key_list = jax.random.split(jax.random.fold_in(key, 202), 6)
    full_shape = (SECTIONS, MB, TOK_ROWS, KC)
    position = jnp.arange(KC, dtype=jnp.float32) / KC
    section_pos = jnp.arange(SECTIONS, dtype=jnp.float32) / max(SECTIONS - 1, 1)
    values = jax.random.normal(key_list[0], full_shape, jnp.float32)
    rising = 3.0 ** (0.5 * position)
    section_scale = 3.0 ** (0.5 * section_pos)
    row_scale = spread_scale(key_list[1], (SECTIONS, MB, TOK_ROWS, 1))
    column_scale = spread_scale(key_list[2], (KC,)) * rising
    noise = values * row_scale * column_scale
    source_cols = jax.random.randint(key_list[4], (8, KC), 0, FEAT)
    mixing = jax.random.normal(key_list[5], (8, KC), jnp.float32)
    shared = jnp.zeros(full_shape, jnp.float32)
    for which in range(8):
        shared = shared + mixing[which] * jnp.take(inputs, source_cols[which], axis=3)
    total = noise + 2.0 / math.sqrt(8.0) * shared
    return (total * section_scale.reshape(SECTIONS, 1, 1, 1)).astype(jnp.bfloat16)


def draw_live_slots(key, part):
    key_list = jax.random.split(key, 4)
    full_one = jax.random.randint(key_list[0], (), 0, SECTIONS)
    random_bits = jax.random.randint(key_list[1], (SECTIONS, MB), 0, 2)
    live_pick = jax.random.randint(key_list[2], (SECTIONS, 1), 0, MB)
    dead_step = jax.random.randint(key_list[3], (SECTIONS, 1), 1, MB)
    dead_pick = (live_pick + dead_step) % MB
    slot_ids = jnp.arange(MB)[None, :]
    forced = jnp.where(slot_ids == live_pick, 1, jnp.where(slot_ids == dead_pick, 0, random_bits))
    full_rows = (jnp.arange(SECTIONS) == full_one)[:, None]
    return jnp.where(full_rows, 1, forced).astype(jnp.int32)


def draw_second_moment(key, part):
    values = jnp.exp(jax.random.uniform(key, (SECTIONS, FEAT, KC), jnp.float32, math.log(0.05), 0.0))
    return values / PARAMS


def steps_of(own_key, extent, cuts, low, high):
    level, own = 1.0, jax.random.fold_in(own_key, 6)
    for axis_at, parts in cuts:
        steps = jnp.exp(jax.random.uniform(jax.random.fold_in(own, axis_at), (parts,), jnp.float32, low / len(cuts), high / len(cuts)))
        level = level * jnp.repeat(steps, extent[axis_at] // parts).reshape([-1 if axis == axis_at else 1 for axis in range(len(extent))])
    return level


def centred(stream_key, shape, deviation, reach, shards=(), kind=jnp.bfloat16):
    entries = jax.random.normal(stream_key, shape, jnp.float32) * deviation
    if len(shards) > 0:
        entries = steps_of(stream_key, shape, shards, -0.22, 0.18) * entries
    return jnp.clip(entries, min=-reach, max=reach).astype(kind)


def setup_inputs(seed: int = 0) -> dict:
    key_of = jax.random.split(jax.random.key(seed), 7)
    normed_input = draw_normed_input(jax.random.fold_in(key_of[6], 71), 0)
    key_grad = draw_key_grad(jax.random.fold_in(key_of[6], 71), 0)
    live_slots = draw_live_slots(jax.random.fold_in(key_of[6], 71), 0)
    master = centred(key_of[3], (SECTIONS, FEAT, KC), 1.0, 4.0, ((0, 2), (1, 8), (2, 2)), jnp.float32)
    first_moment = centred(key_of[4], (SECTIONS, FEAT, KC), (9 * PARAMS) ** -0.5, 0.0009765625, ((0, 2), (1, 8), (2, 2)), jnp.float32)
    second_moment = draw_second_moment(jax.random.fold_in(key_of[6], 71), 0)
    return dict(normed_input=normed_input, key_grad=key_grad, live_slots=live_slots, master=master, first_moment=first_moment, second_moment=second_moment)


MOMENT_DECAY = 0.9
SQUARE_DECAY = 0.95
FIRST_CORRECTION = 1.0 - 0.9 ** 20
SECOND_CORRECTION = 1.0 - 0.95 ** 20
WEIGHT_DECAY = 0.1
CLIP_NORM = 1.0
EPSILON = 1e-08

def section_grad(operands):
    inputs, key_grads, live_row = operands

    def add_slot(running, slot_index):
        term = jnp.dot(inputs[slot_index].T, key_grads[slot_index], preferred_element_type=jnp.float32)
        weight = live_row[slot_index].astype(jnp.float32)
        return (running + weight * term, None)
    running, unused = lax.scan(add_slot, jnp.zeros((FEAT, KC), jnp.float32), jnp.arange(MB, dtype=jnp.int32))
    live_count = jnp.sum(live_row).astype(jnp.int32)
    return running / (live_count * TOK_ROWS).astype(jnp.float32)

def reference(normed_input, key_grad, live_slots, master, first_moment, second_moment):
    grad = lax.map(section_grad, (normed_input, key_grad, live_slots))
    norm = jnp.sqrt(jnp.sum(grad * grad))
    clip_factor = jnp.minimum(1.0, CLIP_NORM / norm)
    clipped = clip_factor * grad
    moment1 = MOMENT_DECAY * first_moment + (1.0 - MOMENT_DECAY) * clipped
    moment2 = SQUARE_DECAY * second_moment + (1.0 - SQUARE_DECAY) * clipped * clipped
    update = moment1 / FIRST_CORRECTION / (jnp.sqrt(moment2 / SECOND_CORRECTION) + EPSILON) + WEIGHT_DECAY * master
    return update.astype(jnp.bfloat16)
```

```python
import jax
import jax.numpy as jnp
from jax import lax
from jax.sharding import PartitionSpec as P

MOMENT_DECAY = 0.9
SQUARE_DECAY = 0.95
FIRST_CORRECTION = 1.0 - 0.9**20
SECOND_CORRECTION = 1.0 - 0.95**20
WEIGHT_DECAY = 0.1
CLIP_NORM = 1.0
EPSILON = 1e-08


def slot_term(inputs, key_grads, live_row, column_count):
    keep_mask = live_row.astype(key_grads.dtype)
    weighted = (key_grads * keep_mask[:, None, None]).reshape(-1, key_grads.shape[2])
    columns = inputs.reshape(-1, column_count)
    return lax.dot_general(
        columns, weighted, (((0,), (0,)), ((), ())), preferred_element_type=jnp.float32
    )


def butterfly_sum(value, axes):
    for axis in axes:
        size = lax.axis_size(axis)
        if size & (size - 1):
            value = lax.psum(value, axis)
            continue
        bit = 1
        while bit < size:
            pairs = [(i, i ^ bit) for i in range(size)]
            value = value + lax.ppermute(value, axis, pairs)
            bit *= 2
    return value


def local(normed_input, key_grad, live_slots, master, first_moment, second_moment):
    inputs = normed_input[0]
    key_grads = key_grad[0]
    live_row = live_slots[0]
    live_count = jnp.sum(live_row)
    features = inputs.shape[2]
    summed = lax.psum_scatter(
        slot_term(inputs, key_grads, live_row, features), "dp", scatter_dimension=0, tiled=True
    )
    tokens_total = (live_count * (inputs.shape[1] * lax.axis_size("dp"))).astype(jnp.float32)
    grad_shard = summed / tokens_total
    squares = butterfly_sum(jnp.sum(grad_shard * grad_shard), ("pipe", "tensor", "dp"))
    clip_factor = jnp.minimum(1.0, CLIP_NORM / jnp.sqrt(squares))
    clipped = clip_factor * grad_shard
    moment1 = MOMENT_DECAY * first_moment[0] + (1.0 - MOMENT_DECAY) * clipped
    moment2 = SQUARE_DECAY * second_moment[0] + (1.0 - SQUARE_DECAY) * clipped * clipped
    update = (
        moment1 / FIRST_CORRECTION / (jnp.sqrt(moment2 / SECOND_CORRECTION) + EPSILON)
        + WEIGHT_DECAY * master[0]
    )
    update_rows = update.astype(jnp.bfloat16)[None]
    return lax.all_gather(update_rows, "dp", axis=1, tiled=True)


def solution(mesh):
    in_specs = (
        P("pipe", None, "dp", None),
        P("pipe", None, "dp", "tensor"),
        P("pipe", None),
        P("pipe", "dp", "tensor"),
        P("pipe", "dp", "tensor"),
        P("pipe", "dp", "tensor"),
    )
    out_specs = P("pipe", None, "tensor")
    return jax.shard_map(local, mesh=mesh, in_specs=in_specs, out_specs=out_specs, check_vma=False)
```

```python
import jax
import jax.numpy as jnp
from jax import lax
from jax.sharding import PartitionSpec as P

MOMENT_DECAY = 0.9
SQUARE_DECAY = 0.95
FIRST_CORRECTION = 1.0 - 0.9**20
SECOND_CORRECTION = 1.0 - 0.95**20
WEIGHT_DECAY = 0.1
CLIP_NORM = 1.0
EPSILON = 1e-08


def slot_term(inputs, key_grads, live_row, column_count):
    keep_mask = live_row.astype(key_grads.dtype)
    weighted = (key_grads * keep_mask[:, None, None]).reshape(-1, key_grads.shape[2])
    columns = inputs.reshape(-1, column_count)
    return lax.dot_general(
        columns, weighted, (((0,), (0,)), ((), ())), preferred_element_type=jnp.float32
    )


def butterfly_sum(value, axes):
    for axis in axes:
        size = lax.axis_size(axis)
        if size & (size - 1):
            value = lax.psum(value, axis)
            continue
        bit = 1
        while bit < size:
            pairs = [(i, i ^ bit) for i in range(size)]
            value = value + lax.ppermute(value, axis, pairs)
            bit *= 2
    return value


def bit_orders(size):
    bits = list(range(size.bit_length() - 1))
    return bits, bits[1:] + bits[:1]


def halving_scatter(partial, axis, order):
    size = lax.axis_size(axis)
    levels = size.bit_length() - 1
    index = lax.axis_index(axis)
    rows, cols = partial.shape
    blocks = partial.reshape((2,) * levels + (rows // size, cols))
    for step, bit in enumerate(order):
        dim = levels - 1 - bit
        dim -= sum(1 for done in order[:step] if levels - 1 - done < dim)
        mine = (index >> bit) & 1
        low = lax.index_in_dim(blocks, 0, dim, keepdims=False)
        high = lax.index_in_dim(blocks, 1, dim, keepdims=False)
        keep = jnp.where(mine == 1, high, low)
        send = jnp.where(mine == 1, low, high)
        pairs = [(i, i ^ (1 << bit)) for i in range(size)]
        blocks = keep + lax.ppermute(send, axis, pairs)
    return blocks.reshape(rows // size, cols)


def doubling_gather(part, axis, order):
    size = lax.axis_size(axis)
    levels = size.bit_length() - 1
    index = lax.axis_index(axis)
    placed = []
    current = part
    for bit in order:
        mine = (index >> bit) & 1
        pairs = [(i, i ^ (1 << bit)) for i in range(size)]
        other = lax.ppermute(current, axis, pairs)
        low = jnp.where(mine == 1, other, current)
        high = jnp.where(mine == 1, current, other)
        current = jnp.stack([low, high], axis=0)
        placed.insert(0, bit)
    perm = [placed.index(bit) for bit in range(levels - 1, -1, -1)]
    current = jnp.transpose(current, perm + list(range(levels, current.ndim)))
    return current.reshape((-1,) + part.shape[1:])


def scatter_rows(partial, axis):
    size = lax.axis_size(axis)
    cols = partial.shape[1]
    if size & (size - 1) or size == 1 or cols % 2:
        return lax.psum_scatter(partial, axis, scatter_dimension=0, tiled=True)
    first, second = bit_orders(size)
    half = cols // 2
    return jnp.concatenate(
        [
            halving_scatter(partial[:, :half], axis, first),
            halving_scatter(partial[:, half:], axis, second),
        ],
        axis=1,
    )


def gather_rows(part, axis):
    size = lax.axis_size(axis)
    cols = part.shape[1]
    if size & (size - 1) or size == 1 or cols % 2:
        return lax.all_gather(part, axis, axis=0, tiled=True)
    first, second = bit_orders(size)
    half = cols // 2
    return jnp.concatenate(
        [
            doubling_gather(part[:, :half], axis, first[::-1]),
            doubling_gather(part[:, half:], axis, second[::-1]),
        ],
        axis=1,
    )


def local(normed_input, key_grad, live_slots, master, first_moment, second_moment):
    inputs = normed_input[0]
    key_grads = key_grad[0]
    live_row = live_slots[0]
    live_count = jnp.sum(live_row)
    features = inputs.shape[2]
    summed = scatter_rows(slot_term(inputs, key_grads, live_row, features), "dp")
    tokens_total = (live_count * (inputs.shape[1] * lax.axis_size("dp"))).astype(jnp.float32)
    grad_shard = summed / tokens_total
    squares = butterfly_sum(jnp.sum(grad_shard * grad_shard), ("pipe", "tensor", "dp"))
    clip_factor = jnp.minimum(1.0, CLIP_NORM / jnp.sqrt(squares))
    clipped = clip_factor * grad_shard
    moment1 = MOMENT_DECAY * first_moment[0] + (1.0 - MOMENT_DECAY) * clipped
    moment2 = SQUARE_DECAY * second_moment[0] + (1.0 - SQUARE_DECAY) * clipped * clipped
    update = (
        moment1 / FIRST_CORRECTION / (jnp.sqrt(moment2 / SECOND_CORRECTION) + EPSILON)
        + WEIGHT_DECAY * master[0]
    )
    return gather_rows(update.astype(jnp.bfloat16), "dp")[None]


def solution(mesh):
    in_specs = (
        P("pipe", None, "dp", None),
        P("pipe", None, "dp", "tensor"),
        P("pipe", None),
        P("pipe", "dp", "tensor"),
        P("pipe", "dp", "tensor"),
        P("pipe", "dp", "tensor"),
    )
    out_specs = P("pipe", None, "tensor")
    return jax.shard_map(local, mesh=mesh, in_specs=in_specs, out_specs=out_specs, check_vma=False)
```

```python
import jax
import jax.numpy as jnp
from jax import lax
from jax.sharding import PartitionSpec as P

MOMENT_DECAY = 0.9
SQUARE_DECAY = 0.95
FIRST_CORRECTION = 1.0 - 0.9**20
SECOND_CORRECTION = 1.0 - 0.95**20
WEIGHT_DECAY = 0.1
CLIP_NORM = 1.0
EPSILON = 1e-08


def slot_term(inputs, key_grads, live_row, column_count):
    keep_mask = live_row.astype(key_grads.dtype)
    weighted = (key_grads * keep_mask[:, None, None]).reshape(-1, key_grads.shape[2])
    columns = inputs.reshape(-1, column_count)
    return lax.dot_general(
        weighted, columns, (((0,), (0,)), ((), ())), preferred_element_type=jnp.float32
    )


def butterfly_sum(value, axes):
    for axis in axes:
        size = lax.axis_size(axis)
        if size & (size - 1):
            value = lax.psum(value, axis)
            continue
        bit = 1
        while bit < size:
            pairs = [(i, i ^ bit) for i in range(size)]
            value = value + lax.ppermute(value, axis, pairs)
            bit *= 2
    return value


def bit_orders(size):
    bits = list(range(size.bit_length() - 1))
    return bits, bits[1:] + bits[:1]


def halving_scatter(partial, axis, order):
    size = lax.axis_size(axis)
    index = lax.axis_index(axis)
    width = partial.shape[1] // size
    held = list(range(size))
    blocks = partial
    for bit in order:
        mine = (index >> bit) & 1
        low = [k for k, block in enumerate(held) if not (block >> bit) & 1]
        high = [k for k, block in enumerate(held) if (block >> bit) & 1]
        low_part = jnp.concatenate([blocks[:, k * width:(k + 1) * width] for k in low], axis=1)
        high_part = jnp.concatenate([blocks[:, k * width:(k + 1) * width] for k in high], axis=1)
        keep = jnp.where(mine == 1, high_part, low_part)
        send = jnp.where(mine == 1, low_part, high_part)
        pairs = [(i, i ^ (1 << bit)) for i in range(size)]
        blocks = keep + lax.ppermute(send, axis, pairs)
        held = [held[k] & ~(1 << bit) for k in low]
    return blocks


def doubling_gather(part, axis, order):
    size = lax.axis_size(axis)
    levels = size.bit_length() - 1
    index = lax.axis_index(axis)
    placed = []
    current = part
    for bit in order:
        mine = (index >> bit) & 1
        pairs = [(i, i ^ (1 << bit)) for i in range(size)]
        other = lax.ppermute(current, axis, pairs)
        low = jnp.where(mine == 1, other, current)
        high = jnp.where(mine == 1, current, other)
        current = jnp.stack([low, high], axis=0)
        placed.insert(0, bit)
    perm = [placed.index(bit) for bit in range(levels - 1, -1, -1)]
    current = jnp.transpose(current, perm + list(range(levels, current.ndim)))
    return current.reshape((-1,) + part.shape[1:])


def scatter_rows(partial_t, axis):
    size = lax.axis_size(axis)
    cols = partial_t.shape[0]
    if size & (size - 1) or size == 1 or cols % 2:
        return lax.psum_scatter(partial_t, axis, scatter_dimension=1, tiled=True)
    first, second = bit_orders(size)
    half = cols // 2
    return jnp.concatenate(
        [
            halving_scatter(partial_t[:half], axis, first),
            halving_scatter(partial_t[half:], axis, second),
        ],
        axis=0,
    )


def gather_rows(part, axis):
    size = lax.axis_size(axis)
    cols = part.shape[1]
    if size & (size - 1) or size == 1 or cols % 2:
        return lax.all_gather(part, axis, axis=0, tiled=True)
    first, second = bit_orders(size)
    half = cols // 2
    return jnp.concatenate(
        [
            doubling_gather(part[:, :half], axis, first[::-1]),
            doubling_gather(part[:, half:], axis, second[::-1]),
        ],
        axis=1,
    )


def local(normed_input, key_grad, live_slots, master, first_moment, second_moment):
    inputs = normed_input[0]
    key_grads = key_grad[0]
    live_row = live_slots[0]
    live_count = jnp.sum(live_row)
    features = inputs.shape[2]
    summed = scatter_rows(slot_term(inputs, key_grads, live_row, features), "dp")
    tokens_total = (live_count * (inputs.shape[1] * lax.axis_size("dp"))).astype(jnp.float32)
    grad_shard = summed / tokens_total
    squares = butterfly_sum(jnp.sum(grad_shard * grad_shard), ("pipe", "tensor", "dp"))
    clip_factor = jnp.minimum(1.0, CLIP_NORM / jnp.sqrt(squares))
    clipped = clip_factor * grad_shard
    moment1 = MOMENT_DECAY * first_moment[0].T + (1.0 - MOMENT_DECAY) * clipped
    moment2 = SQUARE_DECAY * second_moment[0].T + (1.0 - SQUARE_DECAY) * clipped * clipped
    update = (
        moment1 / FIRST_CORRECTION / (jnp.sqrt(moment2 / SECOND_CORRECTION) + EPSILON)
        + WEIGHT_DECAY * master[0].T
    )
    return gather_rows(update.astype(jnp.bfloat16).T, "dp")[None]


def solution(mesh):
    in_specs = (
        P("pipe", None, "dp", None),
        P("pipe", None, "dp", "tensor"),
        P("pipe", None),
        P("pipe", "dp", "tensor"),
        P("pipe", "dp", "tensor"),
        P("pipe", "dp", "tensor"),
    )
    out_specs = P("pipe", None, "tensor")
    return jax.shard_map(local, mesh=mesh, in_specs=in_specs, out_specs=out_specs, check_vma=False)
```

```python
import jax
import jax.numpy as jnp
from jax import lax
from jax.sharding import PartitionSpec as P

MOMENT_DECAY = 0.9
SQUARE_DECAY = 0.95
FIRST_CORRECTION = 1.0 - 0.9**20
SECOND_CORRECTION = 1.0 - 0.95**20
WEIGHT_DECAY = 0.1
CLIP_NORM = 1.0
EPSILON = 1e-08


def slot_term(inputs, key_grads, live_row, column_count):
    keep_mask = live_row.astype(key_grads.dtype)
    weighted = (key_grads * keep_mask[:, None, None]).reshape(-1, key_grads.shape[2])
    columns = inputs.reshape(-1, column_count)
    return lax.dot_general(
        weighted, columns, (((0,), (0,)), ((), ())), preferred_element_type=jnp.float32
    )


def butterfly_sum(value, axes):
    for axis in axes:
        size = lax.axis_size(axis)
        if size & (size - 1):
            value = lax.psum(value, axis)
            continue
        bit = 1
        while bit < size:
            pairs = [(i, i ^ bit) for i in range(size)]
            value = value + lax.ppermute(value, axis, pairs)
            bit *= 2
    return value


def bit_orders(size):
    bits = list(range(size.bit_length() - 1))
    return bits, bits[1:2] + bits[:1] + bits[2:]


def halving_scatter(partial, axis, order):
    size = lax.axis_size(axis)
    index = lax.axis_index(axis)
    width = partial.shape[1] // size
    held = list(range(size))
    blocks = partial
    for bit in order:
        mine = (index >> bit) & 1
        low = [k for k, block in enumerate(held) if not (block >> bit) & 1]
        high = [k for k, block in enumerate(held) if (block >> bit) & 1]
        low_part = jnp.concatenate([blocks[:, k * width:(k + 1) * width] for k in low], axis=1)
        high_part = jnp.concatenate([blocks[:, k * width:(k + 1) * width] for k in high], axis=1)
        keep = jnp.where(mine == 1, high_part, low_part)
        send = jnp.where(mine == 1, low_part, high_part)
        pairs = [(i, i ^ (1 << bit)) for i in range(size)]
        blocks = keep + lax.ppermute(send, axis, pairs)
        held = [held[k] & ~(1 << bit) for k in low]
    return blocks


def doubling_gather(part, axis, order):
    size = lax.axis_size(axis)
    levels = size.bit_length() - 1
    index = lax.axis_index(axis)
    placed = []
    current = part
    for bit in order:
        mine = (index >> bit) & 1
        pairs = [(i, i ^ (1 << bit)) for i in range(size)]
        other = lax.ppermute(current, axis, pairs)
        low = jnp.where(mine == 1, other, current)
        high = jnp.where(mine == 1, current, other)
        current = jnp.stack([low, high], axis=0)
        placed.insert(0, bit)
    perm = [placed.index(bit) for bit in range(levels - 1, -1, -1)]
    current = jnp.transpose(current, perm + list(range(levels, current.ndim)))
    return current.reshape((-1,) + part.shape[1:])


def scatter_rows(partial_t, axis):
    size = lax.axis_size(axis)
    cols = partial_t.shape[0]
    if size & (size - 1) or size == 1 or cols % 2:
        return lax.psum_scatter(partial_t, axis, scatter_dimension=1, tiled=True)
    first, second = bit_orders(size)
    half = cols // 2
    return jnp.concatenate(
        [
            halving_scatter(partial_t[:half], axis, first),
            halving_scatter(partial_t[half:], axis, second),
        ],
        axis=0,
    )


def gather_rows(part, axis):
    size = lax.axis_size(axis)
    cols = part.shape[1]
    if size & (size - 1) or size == 1 or cols % 2:
        return lax.all_gather(part, axis, axis=0, tiled=True)
    first, second = bit_orders(size)
    half = cols // 2
    return jnp.concatenate(
        [
            doubling_gather(part[:, :half], axis, first[::-1]),
            doubling_gather(part[:, half:], axis, second[::-1]),
        ],
        axis=1,
    )


def local(normed_input, key_grad, live_slots, master, first_moment, second_moment):
    inputs = normed_input[0]
    key_grads = key_grad[0]
    live_row = live_slots[0]
    live_count = jnp.sum(live_row)
    features = inputs.shape[2]
    summed = scatter_rows(slot_term(inputs, key_grads, live_row, features), "dp")
    tokens_total = (live_count * (inputs.shape[1] * lax.axis_size("dp"))).astype(jnp.float32)
    grad_shard = summed / tokens_total
    squares = butterfly_sum(jnp.sum(grad_shard * grad_shard), ("pipe", "tensor", "dp"))
    clip_factor = jnp.minimum(1.0, CLIP_NORM / jnp.sqrt(squares))
    clipped = clip_factor * grad_shard
    moment1 = MOMENT_DECAY * first_moment[0].T + (1.0 - MOMENT_DECAY) * clipped
    moment2 = SQUARE_DECAY * second_moment[0].T + (1.0 - SQUARE_DECAY) * clipped * clipped
    update = (
        moment1 / FIRST_CORRECTION / (jnp.sqrt(moment2 / SECOND_CORRECTION) + EPSILON)
        + WEIGHT_DECAY * master[0].T
    )
    return gather_rows(update.astype(jnp.bfloat16).T, "dp")[None]


def solution(mesh):
    in_specs = (
        P("pipe", None, "dp", None),
        P("pipe", None, "dp", "tensor"),
        P("pipe", None),
        P("pipe", "dp", "tensor"),
        P("pipe", "dp", "tensor"),
        P("pipe", "dp", "tensor"),
    )
    out_specs = P("pipe", None, "tensor")
    return jax.shard_map(local, mesh=mesh, in_specs=in_specs, out_specs=out_specs, check_vma=False)
```

```python
import jax
import jax.numpy as jnp
from jax import lax
from jax.sharding import PartitionSpec as P

MOMENT_DECAY = 0.9
SQUARE_DECAY = 0.95
FIRST_CORRECTION = 1.0 - 0.9**20
SECOND_CORRECTION = 1.0 - 0.95**20
WEIGHT_DECAY = 0.1
CLIP_NORM = 1.0
EPSILON = 1e-08


def slot_operands(inputs, key_grads, live_row, column_count):
    keep_mask = live_row.astype(key_grads.dtype)
    weighted = (key_grads * keep_mask[:, None, None]).reshape(-1, key_grads.shape[2])
    return weighted, inputs.reshape(-1, column_count)


def slot_term(weighted, columns):
    return lax.dot_general(
        weighted, columns, (((0,), (0,)), ((), ())), preferred_element_type=jnp.float32
    )


def butterfly_sum(value, axes):
    for axis in axes:
        size = lax.axis_size(axis)
        if size & (size - 1):
            value = lax.psum(value, axis)
            continue
        bit = 1
        while bit < size:
            pairs = [(i, i ^ bit) for i in range(size)]
            value = value + lax.ppermute(value, axis, pairs)
            bit *= 2
    return value


def bit_orders(size):
    bits = list(range(size.bit_length() - 1))
    return bits, bits[1:2] + bits[:1] + bits[2:]


def halving_scatter(partial, axis, order):
    size = lax.axis_size(axis)
    index = lax.axis_index(axis)
    width = partial.shape[1] // size
    held = list(range(size))
    blocks = partial
    for bit in order:
        mine = (index >> bit) & 1
        low = [k for k, block in enumerate(held) if not (block >> bit) & 1]
        high = [k for k, block in enumerate(held) if (block >> bit) & 1]
        low_part = jnp.concatenate([blocks[:, k * width:(k + 1) * width] for k in low], axis=1)
        high_part = jnp.concatenate([blocks[:, k * width:(k + 1) * width] for k in high], axis=1)
        keep = jnp.where(mine == 1, high_part, low_part)
        send = jnp.where(mine == 1, low_part, high_part)
        pairs = [(i, i ^ (1 << bit)) for i in range(size)]
        blocks = keep + lax.ppermute(send, axis, pairs)
        held = [held[k] & ~(1 << bit) for k in low]
    return blocks


def doubling_gather(part, axis, order):
    size = lax.axis_size(axis)
    levels = size.bit_length() - 1
    index = lax.axis_index(axis)
    placed = []
    current = part
    for bit in order:
        mine = (index >> bit) & 1
        pairs = [(i, i ^ (1 << bit)) for i in range(size)]
        other = lax.ppermute(current, axis, pairs)
        low = jnp.where(mine == 1, other, current)
        high = jnp.where(mine == 1, current, other)
        current = jnp.stack([low, high], axis=0)
        placed.insert(0, bit)
    perm = [placed.index(bit) for bit in range(levels - 1, -1, -1)]
    current = jnp.transpose(current, perm + list(range(levels, current.ndim)))
    return current.reshape((-1,) + part.shape[1:])


def scatter_rows(weighted, columns, axis):
    size = lax.axis_size(axis)
    cols = weighted.shape[1]
    if size & (size - 1) or size == 1 or cols % 2:
        partial_t = slot_term(weighted, columns)
        return lax.psum_scatter(partial_t, axis, scatter_dimension=1, tiled=True)
    first, second = bit_orders(size)
    half = cols // 2
    return jnp.concatenate(
        [
            halving_scatter(slot_term(weighted[:, :half], columns), axis, first),
            halving_scatter(slot_term(weighted[:, half:], columns), axis, second),
        ],
        axis=0,
    )


def gather_rows(part, axis):
    size = lax.axis_size(axis)
    cols = part.shape[1]
    if size & (size - 1) or size == 1 or cols % 2:
        return lax.all_gather(part, axis, axis=0, tiled=True)
    first, second = bit_orders(size)
    half = cols // 2
    return jnp.concatenate(
        [
            doubling_gather(part[:, :half], axis, first[::-1]),
            doubling_gather(part[:, half:], axis, second[::-1]),
        ],
        axis=1,
    )


def local(normed_input, key_grad, live_slots, master, first_moment, second_moment):
    inputs = normed_input[0]
    key_grads = key_grad[0]
    live_row = live_slots[0]
    live_count = jnp.sum(live_row)
    features = inputs.shape[2]
    weighted, columns = slot_operands(inputs, key_grads, live_row, features)
    summed = scatter_rows(weighted, columns, "dp")
    tokens_total = (live_count * (inputs.shape[1] * lax.axis_size("dp"))).astype(jnp.float32)
    grad_shard = summed / tokens_total
    squares = butterfly_sum(jnp.sum(grad_shard * grad_shard), ("pipe", "tensor", "dp"))
    clip_factor = jnp.minimum(1.0, CLIP_NORM / jnp.sqrt(squares))
    clipped = clip_factor * grad_shard
    moment1 = MOMENT_DECAY * first_moment[0].T + (1.0 - MOMENT_DECAY) * clipped
    moment2 = SQUARE_DECAY * second_moment[0].T + (1.0 - SQUARE_DECAY) * clipped * clipped
    update = (
        moment1 / FIRST_CORRECTION / (jnp.sqrt(moment2 / SECOND_CORRECTION) + EPSILON)
        + WEIGHT_DECAY * master[0].T
    )
    return gather_rows(update.astype(jnp.bfloat16).T, "dp")[None]


def solution(mesh):
    in_specs = (
        P("pipe", None, "dp", None),
        P("pipe", None, "dp", "tensor"),
        P("pipe", None),
        P("pipe", "dp", "tensor"),
        P("pipe", "dp", "tensor"),
        P("pipe", "dp", "tensor"),
    )
    out_specs = P("pipe", None, "tensor")
    return jax.shard_map(local, mesh=mesh, in_specs=in_specs, out_specs=out_specs, check_vma=False)
```

```python
import jax
import jax.numpy as jnp
from jax import lax
from jax.sharding import PartitionSpec as P

MOMENT_DECAY = 0.9
SQUARE_DECAY = 0.95
FIRST_CORRECTION = 1.0 - 0.9**20
SECOND_CORRECTION = 1.0 - 0.95**20
WEIGHT_DECAY = 0.1
CLIP_NORM = 1.0
EPSILON = 1e-08


def slot_term(inputs, key_grads, live_row, column_count):
    keep_mask = live_row.astype(key_grads.dtype)
    weighted = (key_grads * keep_mask[:, None, None]).reshape(-1, key_grads.shape[2])
    columns = inputs.reshape(-1, column_count)
    return lax.dot_general(
        weighted, columns, (((0,), (0,)), ((), ())), preferred_element_type=jnp.float32
    )


def butterfly_sum(value, axes):
    for axis in axes:
        size = lax.axis_size(axis)
        if size & (size - 1):
            value = lax.psum(value, axis)
            continue
        bit = 1
        while bit < size:
            pairs = [(i, i ^ bit) for i in range(size)]
            value = value + lax.ppermute(value, axis, pairs)
            bit *= 2
    return value


def bit_orders(size):
    bits = list(range(size.bit_length() - 1))
    return bits, bits[1:2] + bits[:1] + bits[2:]


def halving_scatter(partial, axis, order):
    size = lax.axis_size(axis)
    index = lax.axis_index(axis)
    width = partial.shape[1] // size
    held = list(range(size))
    blocks = partial
    for bit in order:
        mine = (index >> bit) & 1
        low = [k for k, block in enumerate(held) if not (block >> bit) & 1]
        high = [k for k, block in enumerate(held) if (block >> bit) & 1]
        low_part = jnp.concatenate([blocks[:, k * width:(k + 1) * width] for k in low], axis=1)
        high_part = jnp.concatenate([blocks[:, k * width:(k + 1) * width] for k in high], axis=1)
        keep = jnp.where(mine == 1, high_part, low_part)
        send = jnp.where(mine == 1, low_part, high_part)
        pairs = [(i, i ^ (1 << bit)) for i in range(size)]
        blocks = keep + lax.ppermute(send, axis, pairs)
        held = [held[k] & ~(1 << bit) for k in low]
    return blocks


def doubling_gather(part, axis, order):
    size = lax.axis_size(axis)
    levels = size.bit_length() - 1
    index = lax.axis_index(axis)
    placed = []
    current = part
    for bit in order:
        mine = (index >> bit) & 1
        pairs = [(i, i ^ (1 << bit)) for i in range(size)]
        other = lax.ppermute(current, axis, pairs)
        low = jnp.where(mine == 1, other, current)
        high = jnp.where(mine == 1, current, other)
        current = jnp.stack([low, high], axis=0)
        placed.insert(0, bit)
    perm = [placed.index(bit) for bit in range(levels - 1, -1, -1)]
    current = jnp.transpose(current, perm + list(range(levels, current.ndim)))
    return current.reshape((-1,) + part.shape[1:])


def scatter_rows(partial_t, axis, parts=4):
    size = lax.axis_size(axis)
    cols = partial_t.shape[0]
    if size & (size - 1) or size == 1 or cols % (8 * parts):
        return lax.psum_scatter(partial_t, axis, scatter_dimension=1, tiled=True)
    orders = bit_orders(size)
    width = cols // parts
    return jnp.concatenate(
        [
            halving_scatter(partial_t[k * width:(k + 1) * width], axis, orders[k % 2])
            for k in range(parts)
        ],
        axis=0,
    )


def gather_rows(part, axis):
    size = lax.axis_size(axis)
    cols = part.shape[1]
    if size & (size - 1) or size == 1 or cols % 2:
        return lax.all_gather(part, axis, axis=0, tiled=True)
    first, second = bit_orders(size)
    half = cols // 2
    return jnp.concatenate(
        [
            doubling_gather(part[:, :half], axis, first[::-1]),
            doubling_gather(part[:, half:], axis, second[::-1]),
        ],
        axis=1,
    )


def local(normed_input, key_grad, live_slots, master, first_moment, second_moment):
    inputs = normed_input[0]
    key_grads = key_grad[0]
    live_row = live_slots[0]
    live_count = jnp.sum(live_row)
    features = inputs.shape[2]
    summed = scatter_rows(slot_term(inputs, key_grads, live_row, features), "dp")
    tokens_total = (live_count * (inputs.shape[1] * lax.axis_size("dp"))).astype(jnp.float32)
    grad_shard = summed / tokens_total
    squares = butterfly_sum(jnp.sum(grad_shard * grad_shard), ("pipe", "tensor", "dp"))
    clip_factor = jnp.minimum(1.0, CLIP_NORM / jnp.sqrt(squares))
    clipped = clip_factor * grad_shard
    moment1 = MOMENT_DECAY * first_moment[0].T + (1.0 - MOMENT_DECAY) * clipped
    moment2 = SQUARE_DECAY * second_moment[0].T + (1.0 - SQUARE_DECAY) * clipped * clipped
    update = (
        moment1 / FIRST_CORRECTION / (jnp.sqrt(moment2 / SECOND_CORRECTION) + EPSILON)
        + WEIGHT_DECAY * master[0].T
    )
    return gather_rows(update.astype(jnp.bfloat16).T, "dp")[None]


def solution(mesh):
    in_specs = (
        P("pipe", None, "dp", None),
        P("pipe", None, "dp", "tensor"),
        P("pipe", None),
        P("pipe", "dp", "tensor"),
        P("pipe", "dp", "tensor"),
        P("pipe", "dp", "tensor"),
    )
    out_specs = P("pipe", None, "tensor")
    return jax.shard_map(local, mesh=mesh, in_specs=in_specs, out_specs=out_specs, check_vma=False)
```

```python
import jax
import jax.numpy as jnp
from jax import lax
from jax.sharding import PartitionSpec as P

MOMENT_DECAY = 0.9
SQUARE_DECAY = 0.95
FIRST_CORRECTION = 1.0 - 0.9**20
SECOND_CORRECTION = 1.0 - 0.95**20
WEIGHT_DECAY = 0.1
CLIP_NORM = 1.0
EPSILON = 1e-08


def slot_term(inputs, key_grads, live_row, column_count):
    keep_mask = live_row.astype(key_grads.dtype)
    weighted = (key_grads * keep_mask[:, None, None]).reshape(-1, key_grads.shape[2])
    columns = inputs.reshape(-1, column_count)
    return lax.dot_general(
        weighted, columns, (((0,), (0,)), ((), ())), preferred_element_type=jnp.float32
    )


def butterfly_sum(value, axes):
    for axis in axes:
        size = lax.axis_size(axis)
        if size & (size - 1):
            value = lax.psum(value, axis)
            continue
        bit = 1
        while bit < size:
            pairs = [(i, i ^ bit) for i in range(size)]
            value = value + lax.ppermute(value, axis, pairs)
            bit *= 2
    return value


def bit_orders(size):
    bits = list(range(size.bit_length() - 1))
    return bits, bits[1:2] + bits[:1] + bits[2:]


def halving_scatter(partial, axis, order):
    size = lax.axis_size(axis)
    index = lax.axis_index(axis)
    width = partial.shape[1] // size
    held = list(range(size))
    blocks = partial
    for bit in order:
        mine = (index >> bit) & 1
        low = [k for k, block in enumerate(held) if not (block >> bit) & 1]
        high = [k for k, block in enumerate(held) if (block >> bit) & 1]
        low_part = jnp.concatenate([blocks[:, k * width:(k + 1) * width] for k in low], axis=1)
        high_part = jnp.concatenate([blocks[:, k * width:(k + 1) * width] for k in high], axis=1)
        keep = jnp.where(mine == 1, high_part, low_part)
        send = jnp.where(mine == 1, low_part, high_part)
        pairs = [(i, i ^ (1 << bit)) for i in range(size)]
        blocks = keep + lax.ppermute(send, axis, pairs)
        held = [held[k] & ~(1 << bit) for k in low]
    return blocks


def doubling_gather(part, axis, order):
    size = lax.axis_size(axis)
    levels = size.bit_length() - 1
    index = lax.axis_index(axis)
    placed = []
    current = part
    for bit in order:
        mine = (index >> bit) & 1
        pairs = [(i, i ^ (1 << bit)) for i in range(size)]
        other = lax.ppermute(current, axis, pairs)
        low = jnp.where(mine == 1, other, current)
        high = jnp.where(mine == 1, current, other)
        current = jnp.stack([low, high], axis=0)
        placed.insert(0, bit)
    perm = [placed.index(bit) for bit in range(levels - 1, -1, -1)]
    current = jnp.transpose(current, perm + list(range(levels, current.ndim)))
    return current.reshape((-1,) + part.shape[1:])


def scatter_rows(partial_t, axis, parts=8):
    size = lax.axis_size(axis)
    cols = partial_t.shape[0]
    if size & (size - 1) or size == 1 or cols % (8 * parts):
        return lax.psum_scatter(partial_t, axis, scatter_dimension=1, tiled=True)
    orders = bit_orders(size)
    width = cols // parts
    return jnp.concatenate(
        [
            halving_scatter(partial_t[k * width:(k + 1) * width], axis, orders[k % 2])
            for k in range(parts)
        ],
        axis=0,
    )


def gather_rows(part, axis):
    size = lax.axis_size(axis)
    cols = part.shape[1]
    if size & (size - 1) or size == 1 or cols % 2:
        return lax.all_gather(part, axis, axis=0, tiled=True)
    first, second = bit_orders(size)
    half = cols // 2
    return jnp.concatenate(
        [
            doubling_gather(part[:, :half], axis, first[::-1]),
            doubling_gather(part[:, half:], axis, second[::-1]),
        ],
        axis=1,
    )


def local(normed_input, key_grad, live_slots, master, first_moment, second_moment):
    inputs = normed_input[0]
    key_grads = key_grad[0]
    live_row = live_slots[0]
    live_count = jnp.sum(live_row)
    features = inputs.shape[2]
    summed = scatter_rows(slot_term(inputs, key_grads, live_row, features), "dp")
    tokens_total = (live_count * (inputs.shape[1] * lax.axis_size("dp"))).astype(jnp.float32)
    grad_shard = summed / tokens_total
    squares = butterfly_sum(jnp.sum(grad_shard * grad_shard), ("pipe", "tensor", "dp"))
    clip_factor = jnp.minimum(1.0, CLIP_NORM / jnp.sqrt(squares))
    clipped = clip_factor * grad_shard
    moment1 = MOMENT_DECAY * first_moment[0].T + (1.0 - MOMENT_DECAY) * clipped
    moment2 = SQUARE_DECAY * second_moment[0].T + (1.0 - SQUARE_DECAY) * clipped * clipped
    update = (
        moment1 / FIRST_CORRECTION / (jnp.sqrt(moment2 / SECOND_CORRECTION) + EPSILON)
        + WEIGHT_DECAY * master[0].T
    )
    return gather_rows(update.astype(jnp.bfloat16).T, "dp")[None]


def solution(mesh):
    in_specs = (
        P("pipe", None, "dp", None),
        P("pipe", None, "dp", "tensor"),
        P("pipe", None),
        P("pipe", "dp", "tensor"),
        P("pipe", "dp", "tensor"),
        P("pipe", "dp", "tensor"),
    )
    out_specs = P("pipe", None, "tensor")
    return jax.shard_map(local, mesh=mesh, in_specs=in_specs, out_specs=out_specs, check_vma=False)
```

```python
import jax
import jax.numpy as jnp
from jax import lax
from jax.sharding import PartitionSpec as P

MOMENT_DECAY = 0.9
SQUARE_DECAY = 0.95
FIRST_CORRECTION = 1.0 - 0.9**20
SECOND_CORRECTION = 1.0 - 0.95**20
WEIGHT_DECAY = 0.1
CLIP_NORM = 1.0
EPSILON = 1e-08


def slot_term(inputs, key_grads, live_row, column_count):
    keep_mask = live_row.astype(key_grads.dtype)
    weighted = (key_grads * keep_mask[:, None, None]).reshape(-1, key_grads.shape[2])
    columns = inputs.reshape(-1, column_count)
    return lax.dot_general(
        weighted, columns, (((0,), (0,)), ((), ())), preferred_element_type=jnp.float32
    )


def butterfly_sum(value, axes):
    for axis in axes:
        size = lax.axis_size(axis)
        if size & (size - 1):
            value = lax.psum(value, axis)
            continue
        bit = 1
        while bit < size:
            pairs = [(i, i ^ bit) for i in range(size)]
            value = value + lax.ppermute(value, axis, pairs)
            bit *= 2
    return value


def bit_orders(size):
    bits = list(range(size.bit_length() - 1))
    return bits, bits[1:2] + bits[:1] + bits[2:]


def halving_scatter(partial, axis, order):
    size = lax.axis_size(axis)
    index = lax.axis_index(axis)
    width = partial.shape[1] // size
    held = list(range(size))
    blocks = partial
    for bit in order:
        mine = (index >> bit) & 1
        low = [k for k, block in enumerate(held) if not (block >> bit) & 1]
        high = [k for k, block in enumerate(held) if (block >> bit) & 1]
        low_part = jnp.concatenate([blocks[:, k * width:(k + 1) * width] for k in low], axis=1)
        high_part = jnp.concatenate([blocks[:, k * width:(k + 1) * width] for k in high], axis=1)
        keep = jnp.where(mine == 1, high_part, low_part)
        send = jnp.where(mine == 1, low_part, high_part)
        pairs = [(i, i ^ (1 << bit)) for i in range(size)]
        blocks = keep + lax.ppermute(send, axis, pairs)
        held = [held[k] & ~(1 << bit) for k in low]
    return blocks


def doubling_gather(part, axis, order):
    size = lax.axis_size(axis)
    index = lax.axis_index(axis)
    width = part.shape[1]
    held = [0]
    blocks = part
    for bit in order:
        mine = (index >> bit) & 1
        pairs = [(i, i ^ (1 << bit)) for i in range(size)]
        other = lax.ppermute(blocks, axis, pairs)
        low = jnp.where(mine == 1, other, blocks)
        high = jnp.where(mine == 1, blocks, other)
        merged = sorted([(block, 0, k) for k, block in enumerate(held)] + [(block | (1 << bit), 1, k) for k, block in enumerate(held)])
        blocks = jnp.concatenate(
            [(high if side else low)[:, k * width:(k + 1) * width] for _, side, k in merged], axis=1
        )
        held = [block for block, _, _ in merged]
    return blocks


def scatter_rows(partial_t, axis, parts=4):
    size = lax.axis_size(axis)
    cols = partial_t.shape[0]
    if size & (size - 1) or size == 1 or cols % (8 * parts):
        return lax.psum_scatter(partial_t, axis, scatter_dimension=1, tiled=True)
    orders = bit_orders(size)
    width = cols // parts
    return jnp.concatenate(
        [
            halving_scatter(partial_t[k * width:(k + 1) * width], axis, orders[k % 2])
            for k in range(parts)
        ],
        axis=0,
    )


def gather_rows(part_t, axis, parts=4):
    size = lax.axis_size(axis)
    cols = part_t.shape[0]
    if size & (size - 1) or size == 1 or cols % (16 * parts):
        return lax.all_gather(part_t.T, axis, axis=0, tiled=True)
    orders = bit_orders(size)
    width = cols // parts
    return jnp.concatenate(
        [
            doubling_gather(part_t[k * width:(k + 1) * width], axis, orders[k % 2][::-1])
            for k in range(parts)
        ],
        axis=0,
    ).T


def local(normed_input, key_grad, live_slots, master, first_moment, second_moment):
    inputs = normed_input[0]
    key_grads = key_grad[0]
    live_row = live_slots[0]
    live_count = jnp.sum(live_row)
    features = inputs.shape[2]
    summed = scatter_rows(slot_term(inputs, key_grads, live_row, features), "dp")
    tokens_total = (live_count * (inputs.shape[1] * lax.axis_size("dp"))).astype(jnp.float32)
    grad_shard = summed / tokens_total
    squares = butterfly_sum(jnp.sum(grad_shard * grad_shard), ("pipe", "tensor", "dp"))
    clip_factor = jnp.minimum(1.0, CLIP_NORM / jnp.sqrt(squares))
    clipped = clip_factor * grad_shard
    moment1 = MOMENT_DECAY * first_moment[0].T + (1.0 - MOMENT_DECAY) * clipped
    moment2 = SQUARE_DECAY * second_moment[0].T + (1.0 - SQUARE_DECAY) * clipped * clipped
    update = (
        moment1 / FIRST_CORRECTION / (jnp.sqrt(moment2 / SECOND_CORRECTION) + EPSILON)
        + WEIGHT_DECAY * master[0].T
    )
    return gather_rows(update.astype(jnp.bfloat16), "dp")[None]


def solution(mesh):
    in_specs = (
        P("pipe", None, "dp", None),
        P("pipe", None, "dp", "tensor"),
        P("pipe", None),
        P("pipe", "dp", "tensor"),
        P("pipe", "dp", "tensor"),
        P("pipe", "dp", "tensor"),
    )
    out_specs = P("pipe", None, "tensor")
    return jax.shard_map(local, mesh=mesh, in_specs=in_specs, out_specs=out_specs, check_vma=False)
```

```python
import jax
import jax.numpy as jnp
from jax import lax
from jax.sharding import PartitionSpec as P

MOMENT_DECAY = 0.9
SQUARE_DECAY = 0.95
FIRST_CORRECTION = 1.0 - 0.9**20
SECOND_CORRECTION = 1.0 - 0.95**20
WEIGHT_DECAY = 0.1
CLIP_NORM = 1.0
EPSILON = 1e-08


def slot_term(inputs, key_grads, live_row, column_count):
    keep_mask = live_row.astype(key_grads.dtype)
    weighted = (key_grads * keep_mask[:, None, None]).reshape(-1, key_grads.shape[2])
    columns = inputs.reshape(-1, column_count)
    return lax.dot_general(
        weighted, columns, (((0,), (0,)), ((), ())), preferred_element_type=jnp.float32
    )


def butterfly_sum(value, axes):
    for axis in axes:
        size = lax.axis_size(axis)
        if size & (size - 1):
            value = lax.psum(value, axis)
            continue
        bit = 1
        while bit < size:
            pairs = [(i, i ^ bit) for i in range(size)]
            value = value + lax.ppermute(value, axis, pairs)
            bit *= 2
    return value


def bit_orders(size):
    bits = list(range(size.bit_length() - 1))
    return bits, bits[1:2] + bits[:1] + bits[2:]


def halving_scatter(partial, axis, order):
    size = lax.axis_size(axis)
    index = lax.axis_index(axis)
    width = partial.shape[1] // size
    held = list(range(size))
    blocks = partial
    for bit in order:
        mine = (index >> bit) & 1
        low = [k for k, block in enumerate(held) if not (block >> bit) & 1]
        high = [k for k, block in enumerate(held) if (block >> bit) & 1]
        low_part = jnp.concatenate([blocks[:, k * width:(k + 1) * width] for k in low], axis=1)
        high_part = jnp.concatenate([blocks[:, k * width:(k + 1) * width] for k in high], axis=1)
        keep = jnp.where(mine == 1, high_part, low_part)
        send = jnp.where(mine == 1, low_part, high_part)
        pairs = [(i, i ^ (1 << bit)) for i in range(size)]
        blocks = keep + lax.ppermute(send, axis, pairs)
        held = [held[k] & ~(1 << bit) for k in low]
    return blocks


def doubling_gather(part, axis, order):
    size = lax.axis_size(axis)
    levels = size.bit_length() - 1
    index = lax.axis_index(axis)
    placed = []
    current = part
    for bit in order:
        mine = (index >> bit) & 1
        pairs = [(i, i ^ (1 << bit)) for i in range(size)]
        other = lax.ppermute(current, axis, pairs)
        low = jnp.where(mine == 1, other, current)
        high = jnp.where(mine == 1, current, other)
        current = jnp.stack([low, high], axis=0)
        placed.insert(0, bit)
    perm = [placed.index(bit) for bit in range(levels - 1, -1, -1)]
    current = jnp.transpose(current, perm + list(range(levels, current.ndim)))
    return current.reshape((-1,) + part.shape[1:])


def scatter_rows(partial_t, axis, parts=4):
    size = lax.axis_size(axis)
    cols = partial_t.shape[0]
    if size & (size - 1) or size == 1 or cols % (8 * parts):
        return lax.psum_scatter(partial_t, axis, scatter_dimension=1, tiled=True)
    orders = bit_orders(size)
    width = cols // parts
    return jnp.concatenate(
        [
            halving_scatter(partial_t[k * width:(k + 1) * width], axis, orders[int(k % 4 == 1)])
            for k in range(parts)
        ],
        axis=0,
    )


def gather_rows(part, axis):
    size = lax.axis_size(axis)
    cols = part.shape[1]
    if size & (size - 1) or size == 1 or cols % 2:
        return lax.all_gather(part, axis, axis=0, tiled=True)
    first, second = bit_orders(size)
    half = cols // 2
    return jnp.concatenate(
        [
            doubling_gather(part[:, :half], axis, first[::-1]),
            doubling_gather(part[:, half:], axis, second[::-1]),
        ],
        axis=1,
    )


def local(normed_input, key_grad, live_slots, master, first_moment, second_moment):
    inputs = normed_input[0]
    key_grads = key_grad[0]
    live_row = live_slots[0]
    live_count = jnp.sum(live_row)
    features = inputs.shape[2]
    summed = scatter_rows(slot_term(inputs, key_grads, live_row, features), "dp")
    tokens_total = (live_count * (inputs.shape[1] * lax.axis_size("dp"))).astype(jnp.float32)
    grad_shard = summed / tokens_total
    squares = butterfly_sum(jnp.sum(grad_shard * grad_shard), ("pipe", "tensor", "dp"))
    clip_factor = jnp.minimum(1.0, CLIP_NORM / jnp.sqrt(squares))
    clipped = clip_factor * grad_shard
    moment1 = MOMENT_DECAY * first_moment[0].T + (1.0 - MOMENT_DECAY) * clipped
    moment2 = SQUARE_DECAY * second_moment[0].T + (1.0 - SQUARE_DECAY) * clipped * clipped
    update = (
        moment1 / FIRST_CORRECTION / (jnp.sqrt(moment2 / SECOND_CORRECTION) + EPSILON)
        + WEIGHT_DECAY * master[0].T
    )
    return gather_rows(update.astype(jnp.bfloat16).T, "dp")[None]


def solution(mesh):
    in_specs = (
        P("pipe", None, "dp", None),
        P("pipe", None, "dp", "tensor"),
        P("pipe", None),
        P("pipe", "dp", "tensor"),
        P("pipe", "dp", "tensor"),
        P("pipe", "dp", "tensor"),
    )
    out_specs = P("pipe", None, "tensor")
    return jax.shard_map(local, mesh=mesh, in_specs=in_specs, out_specs=out_specs, check_vma=False)
```

```python
import jax
import jax.numpy as jnp
from jax import lax
from jax.sharding import PartitionSpec as P

MOMENT_DECAY = 0.9
SQUARE_DECAY = 0.95
FIRST_CORRECTION = 1.0 - 0.9**20
SECOND_CORRECTION = 1.0 - 0.95**20
WEIGHT_DECAY = 0.1
CLIP_NORM = 1.0
EPSILON = 1e-08


def slot_term(inputs, key_grads, live_row, column_count):
    keep_mask = live_row.astype(key_grads.dtype)
    weighted = (key_grads * keep_mask[:, None, None]).reshape(-1, key_grads.shape[2])
    columns = inputs.reshape(-1, column_count)
    return lax.dot_general(
        weighted, columns, (((0,), (0,)), ((), ())), preferred_element_type=jnp.float32
    )


def butterfly_sum(value, axes):
    for axis in axes:
        size = lax.axis_size(axis)
        if size & (size - 1) or axis == "pipe":
            value = lax.psum(value, axis)
            continue
        bit = 1
        while bit < size:
            pairs = [(i, i ^ bit) for i in range(size)]
            value = value + lax.ppermute(value, axis, pairs)
            bit *= 2
    return value


def bit_orders(size):
    bits = list(range(size.bit_length() - 1))
    return bits, bits[1:2] + bits[:1] + bits[2:]


def halving_scatter(partial, axis, order):
    size = lax.axis_size(axis)
    index = lax.axis_index(axis)
    width = partial.shape[1] // size
    held = list(range(size))
    blocks = partial
    for bit in order:
        mine = (index >> bit) & 1
        low = [k for k, block in enumerate(held) if not (block >> bit) & 1]
        high = [k for k, block in enumerate(held) if (block >> bit) & 1]
        low_part = jnp.concatenate([blocks[:, k * width:(k + 1) * width] for k in low], axis=1)
        high_part = jnp.concatenate([blocks[:, k * width:(k + 1) * width] for k in high], axis=1)
        keep = jnp.where(mine == 1, high_part, low_part)
        send = jnp.where(mine == 1, low_part, high_part)
        pairs = [(i, i ^ (1 << bit)) for i in range(size)]
        blocks = keep + lax.ppermute(send, axis, pairs)
        held = [held[k] & ~(1 << bit) for k in low]
    return blocks


def doubling_gather(part, axis, order):
    size = lax.axis_size(axis)
    levels = size.bit_length() - 1
    index = lax.axis_index(axis)
    placed = []
    current = part
    for bit in order:
        mine = (index >> bit) & 1
        pairs = [(i, i ^ (1 << bit)) for i in range(size)]
        other = lax.ppermute(current, axis, pairs)
        low = jnp.where(mine == 1, other, current)
        high = jnp.where(mine == 1, current, other)
        current = jnp.stack([low, high], axis=0)
        placed.insert(0, bit)
    perm = [placed.index(bit) for bit in range(levels - 1, -1, -1)]
    current = jnp.transpose(current, perm + list(range(levels, current.ndim)))
    return current.reshape((-1,) + part.shape[1:])


def scatter_rows(partial_t, axis, parts=4):
    size = lax.axis_size(axis)
    cols = partial_t.shape[0]
    if size & (size - 1) or size == 1 or cols % (8 * parts):
        return lax.psum_scatter(partial_t, axis, scatter_dimension=1, tiled=True)
    orders = bit_orders(size)
    width = cols // parts
    return jnp.concatenate(
        [
            halving_scatter(partial_t[k * width:(k + 1) * width], axis, orders[k % 2])
            for k in range(parts)
        ],
        axis=0,
    )


def gather_rows(part, axis):
    size = lax.axis_size(axis)
    cols = part.shape[1]
    if size & (size - 1) or size == 1 or cols % 2:
        return lax.all_gather(part, axis, axis=0, tiled=True)
    first, second = bit_orders(size)
    half = cols // 2
    return jnp.concatenate(
        [
            doubling_gather(part[:, :half], axis, first[::-1]),
            doubling_gather(part[:, half:], axis, second[::-1]),
        ],
        axis=1,
    )


def local(normed_input, key_grad, live_slots, master, first_moment, second_moment):
    inputs = normed_input[0]
    key_grads = key_grad[0]
    live_row = live_slots[0]
    live_count = jnp.sum(live_row)
    features = inputs.shape[2]
    summed = scatter_rows(slot_term(inputs, key_grads, live_row, features), "dp")
    tokens_total = (live_count * (inputs.shape[1] * lax.axis_size("dp"))).astype(jnp.float32)
    grad_shard = summed / tokens_total
    squares = butterfly_sum(jnp.sum(grad_shard * grad_shard), ("pipe", "tensor", "dp"))
    clip_factor = jnp.minimum(1.0, CLIP_NORM / jnp.sqrt(squares))
    clipped = clip_factor * grad_shard
    moment1 = MOMENT_DECAY * first_moment[0].T + (1.0 - MOMENT_DECAY) * clipped
    moment2 = SQUARE_DECAY * second_moment[0].T + (1.0 - SQUARE_DECAY) * clipped * clipped
    update = (
        moment1 / FIRST_CORRECTION / (jnp.sqrt(moment2 / SECOND_CORRECTION) + EPSILON)
        + WEIGHT_DECAY * master[0].T
    )
    return gather_rows(update.astype(jnp.bfloat16).T, "dp")[None]


def solution(mesh):
    in_specs = (
        P("pipe", None, "dp", None),
        P("pipe", None, "dp", "tensor"),
        P("pipe", None),
        P("pipe", "dp", "tensor"),
        P("pipe", "dp", "tensor"),
        P("pipe", "dp", "tensor"),
    )
    out_specs = P("pipe", None, "tensor")
    return jax.shard_map(local, mesh=mesh, in_specs=in_specs, out_specs=out_specs, check_vma=False)
```

```python
import jax
import jax.numpy as jnp
from jax import lax
from jax.sharding import PartitionSpec as P

MOMENT_DECAY = 0.9
SQUARE_DECAY = 0.95
FIRST_CORRECTION = 1.0 - 0.9**20
SECOND_CORRECTION = 1.0 - 0.95**20
WEIGHT_DECAY = 0.1
CLIP_NORM = 1.0
EPSILON = 1e-08


def slot_term(inputs, key_grads, live_row, column_count):
    keep_mask = live_row.astype(key_grads.dtype)
    weighted = (key_grads * keep_mask[:, None, None]).reshape(-1, key_grads.shape[2])
    columns = inputs.reshape(-1, column_count)
    return lax.dot_general(
        weighted, columns, (((0,), (0,)), ((), ())), preferred_element_type=jnp.float32
    )


def butterfly_sum(value, axes):
    for axis in axes:
        size = lax.axis_size(axis)
        if size & (size - 1):
            value = lax.psum(value, axis)
            continue
        bit = 1
        while bit < size:
            pairs = [(i, i ^ bit) for i in range(size)]
            value = value + lax.ppermute(value, axis, pairs)
            bit *= 2
    return value


def bit_orders(size):
    bits = list(range(size.bit_length() - 1))
    return bits, bits[1:2] + bits[:1] + bits[2:], bits[:1] + bits[2:3] + bits[1:2] + bits[3:]


def halving_scatter(partial, axis, order):
    size = lax.axis_size(axis)
    index = lax.axis_index(axis)
    width = partial.shape[1] // size
    held = list(range(size))
    blocks = partial
    for bit in order:
        mine = (index >> bit) & 1
        low = [k for k, block in enumerate(held) if not (block >> bit) & 1]
        high = [k for k, block in enumerate(held) if (block >> bit) & 1]
        low_part = jnp.concatenate([blocks[:, k * width:(k + 1) * width] for k in low], axis=1)
        high_part = jnp.concatenate([blocks[:, k * width:(k + 1) * width] for k in high], axis=1)
        keep = jnp.where(mine == 1, high_part, low_part)
        send = jnp.where(mine == 1, low_part, high_part)
        pairs = [(i, i ^ (1 << bit)) for i in range(size)]
        blocks = keep + lax.ppermute(send, axis, pairs)
        held = [held[k] & ~(1 << bit) for k in low]
    return blocks


def doubling_gather(part, axis, order):
    size = lax.axis_size(axis)
    levels = size.bit_length() - 1
    index = lax.axis_index(axis)
    placed = []
    current = part
    for bit in order:
        mine = (index >> bit) & 1
        pairs = [(i, i ^ (1 << bit)) for i in range(size)]
        other = lax.ppermute(current, axis, pairs)
        low = jnp.where(mine == 1, other, current)
        high = jnp.where(mine == 1, current, other)
        current = jnp.stack([low, high], axis=0)
        placed.insert(0, bit)
    perm = [placed.index(bit) for bit in range(levels - 1, -1, -1)]
    current = jnp.transpose(current, perm + list(range(levels, current.ndim)))
    return current.reshape((-1,) + part.shape[1:])


def scatter_rows(partial_t, axis, parts=4):
    size = lax.axis_size(axis)
    cols = partial_t.shape[0]
    if size & (size - 1) or size == 1 or cols % (8 * parts):
        return lax.psum_scatter(partial_t, axis, scatter_dimension=1, tiled=True)
    orders = bit_orders(size)
    width = cols // parts
    return jnp.concatenate(
        [
            halving_scatter(partial_t[k * width:(k + 1) * width], axis, orders[(0, 1, 2, 1)[k % 4]])
            for k in range(parts)
        ],
        axis=0,
    )


def gather_rows(part, axis):
    size = lax.axis_size(axis)
    cols = part.shape[1]
    if size & (size - 1) or size == 1 or cols % 2:
        return lax.all_gather(part, axis, axis=0, tiled=True)
    first, second = bit_orders(size)[:2]
    half = cols // 2
    return jnp.concatenate(
        [
            doubling_gather(part[:, :half], axis, first[::-1]),
            doubling_gather(part[:, half:], axis, second[::-1]),
        ],
        axis=1,
    )


def local(normed_input, key_grad, live_slots, master, first_moment, second_moment):
    inputs = normed_input[0]
    key_grads = key_grad[0]
    live_row = live_slots[0]
    live_count = jnp.sum(live_row)
    features = inputs.shape[2]
    summed = scatter_rows(slot_term(inputs, key_grads, live_row, features), "dp")
    tokens_total = (live_count * (inputs.shape[1] * lax.axis_size("dp"))).astype(jnp.float32)
    grad_shard = summed / tokens_total
    squares = butterfly_sum(jnp.sum(grad_shard * grad_shard), ("pipe", "tensor", "dp"))
    clip_factor = jnp.minimum(1.0, CLIP_NORM / jnp.sqrt(squares))
    clipped = clip_factor * grad_shard
    moment1 = MOMENT_DECAY * first_moment[0].T + (1.0 - MOMENT_DECAY) * clipped
    moment2 = SQUARE_DECAY * second_moment[0].T + (1.0 - SQUARE_DECAY) * clipped * clipped
    update = (
        moment1 / FIRST_CORRECTION / (jnp.sqrt(moment2 / SECOND_CORRECTION) + EPSILON)
        + WEIGHT_DECAY * master[0].T
    )
    return gather_rows(update.astype(jnp.bfloat16).T, "dp")[None]


def solution(mesh):
    in_specs = (
        P("pipe", None, "dp", None),
        P("pipe", None, "dp", "tensor"),
        P("pipe", None),
        P("pipe", "dp", "tensor"),
        P("pipe", "dp", "tensor"),
        P("pipe", "dp", "tensor"),
    )
    out_specs = P("pipe", None, "tensor")
    return jax.shard_map(local, mesh=mesh, in_specs=in_specs, out_specs=out_specs, check_vma=False)
```

```python
import jax
import jax.numpy as jnp
from jax import lax
from jax.sharding import PartitionSpec as P

MOMENT_DECAY = 0.9
SQUARE_DECAY = 0.95
FIRST_CORRECTION = 1.0 - 0.9**20
SECOND_CORRECTION = 1.0 - 0.95**20
WEIGHT_DECAY = 0.1
CLIP_NORM = 1.0
EPSILON = 1e-08


def slot_term(inputs, key_grads, live_row, column_count):
    keep_mask = live_row.astype(key_grads.dtype)
    weighted = (key_grads * keep_mask[:, None, None]).reshape(-1, key_grads.shape[2])
    columns = inputs.reshape(-1, column_count)
    return lax.dot_general(
        weighted, columns, (((0,), (0,)), ((), ())), preferred_element_type=jnp.float32
    )


def butterfly_sum(value, axes):
    for axis in axes:
        size = lax.axis_size(axis)
        if size & (size - 1):
            value = lax.psum(value, axis)
            continue
        bit = 1
        while bit < size:
            pairs = [(i, i ^ bit) for i in range(size)]
            value = value + lax.ppermute(value, axis, pairs)
            bit *= 2
    return value


def bit_orders(size):
    bits = list(range(size.bit_length() - 1))
    return bits, bits[1:2] + bits[:1] + bits[2:], bits[:1] + bits[2:3] + bits[1:2] + bits[3:]


def halving_scatter(partial, axis, order):
    size = lax.axis_size(axis)
    index = lax.axis_index(axis)
    width = partial.shape[1] // size
    held = list(range(size))
    blocks = partial
    for bit in order:
        mine = (index >> bit) & 1
        low = [k for k, block in enumerate(held) if not (block >> bit) & 1]
        high = [k for k, block in enumerate(held) if (block >> bit) & 1]
        low_part = jnp.concatenate([blocks[:, k * width:(k + 1) * width] for k in low], axis=1)
        high_part = jnp.concatenate([blocks[:, k * width:(k + 1) * width] for k in high], axis=1)
        keep = jnp.where(mine == 1, high_part, low_part)
        send = jnp.where(mine == 1, low_part, high_part)
        pairs = [(i, i ^ (1 << bit)) for i in range(size)]
        blocks = keep + lax.ppermute(send, axis, pairs)
        held = [held[k] & ~(1 << bit) for k in low]
    return blocks


def doubling_gather(part, axis, order):
    size = lax.axis_size(axis)
    levels = size.bit_length() - 1
    index = lax.axis_index(axis)
    placed = []
    current = part
    for bit in order:
        mine = (index >> bit) & 1
        pairs = [(i, i ^ (1 << bit)) for i in range(size)]
        other = lax.ppermute(current, axis, pairs)
        low = jnp.where(mine == 1, other, current)
        high = jnp.where(mine == 1, current, other)
        current = jnp.stack([low, high], axis=0)
        placed.insert(0, bit)
    perm = [placed.index(bit) for bit in range(levels - 1, -1, -1)]
    current = jnp.transpose(current, perm + list(range(levels, current.ndim)))
    return current.reshape((-1,) + part.shape[1:])


def scatter_rows(partial_t, axis, parts=4):
    size = lax.axis_size(axis)
    cols = partial_t.shape[0]
    if size & (size - 1) or size == 1 or cols % (8 * parts):
        return lax.psum_scatter(partial_t, axis, scatter_dimension=1, tiled=True)
    orders = bit_orders(size)
    width = cols // parts
    return jnp.concatenate(
        [
            halving_scatter(partial_t[k * width:(k + 1) * width], axis, orders[(0, 1, 2, 1)[k % 4]])
            for k in range(parts)
        ],
        axis=0,
    )


def gather_rows(part, axis):
    size = lax.axis_size(axis)
    rows, cols = part.shape
    if size & (size - 1) or size == 1 or cols % 256 or rows % 32:
        return lax.all_gather(part, axis, axis=0, tiled=True)
    first, second = bit_orders(size)[:2]
    half_rows, half_cols = rows // 2, cols // 2
    columns = []
    for h in range(2):
        gathered = []
        for r in range(2):
            piece = part[r * half_rows:(r + 1) * half_rows, h * half_cols:(h + 1) * half_cols]
            order = (first, second)[(h + r) % 2][::-1]
            gathered.append(doubling_gather(piece, axis, order).reshape(size, half_rows, half_cols))
        columns.append(jnp.stack(gathered, axis=1).reshape(size * rows, half_cols))
    return jnp.concatenate(columns, axis=1)


def local(normed_input, key_grad, live_slots, master, first_moment, second_moment):
    inputs = normed_input[0]
    key_grads = key_grad[0]
    live_row = live_slots[0]
    live_count = jnp.sum(live_row)
    features = inputs.shape[2]
    summed = scatter_rows(slot_term(inputs, key_grads, live_row, features), "dp")
    tokens_total = (live_count * (inputs.shape[1] * lax.axis_size("dp"))).astype(jnp.float32)
    grad_shard = summed / tokens_total
    squares = butterfly_sum(jnp.sum(grad_shard * grad_shard), ("pipe", "tensor", "dp"))
    clip_factor = jnp.minimum(1.0, CLIP_NORM / jnp.sqrt(squares))
    clipped = clip_factor * grad_shard
    moment1 = MOMENT_DECAY * first_moment[0].T + (1.0 - MOMENT_DECAY) * clipped
    moment2 = SQUARE_DECAY * second_moment[0].T + (1.0 - SQUARE_DECAY) * clipped * clipped
    update = (
        moment1 / FIRST_CORRECTION / (jnp.sqrt(moment2 / SECOND_CORRECTION) + EPSILON)
        + WEIGHT_DECAY * master[0].T
    )
    return gather_rows(update.astype(jnp.bfloat16).T, "dp")[None]


def solution(mesh):
    in_specs = (
        P("pipe", None, "dp", None),
        P("pipe", None, "dp", "tensor"),
        P("pipe", None),
        P("pipe", "dp", "tensor"),
        P("pipe", "dp", "tensor"),
        P("pipe", "dp", "tensor"),
    )
    out_specs = P("pipe", None, "tensor")
    return jax.shard_map(local, mesh=mesh, in_specs=in_specs, out_specs=out_specs, check_vma=False)
```

```python
import jax
import jax.numpy as jnp
from jax import lax
from jax.sharding import PartitionSpec as P

MOMENT_DECAY = 0.9
SQUARE_DECAY = 0.95
FIRST_CORRECTION = 1.0 - 0.9**20
SECOND_CORRECTION = 1.0 - 0.95**20
WEIGHT_DECAY = 0.1
CLIP_NORM = 1.0
EPSILON = 1e-08


def slot_term(inputs, key_grads, live_row, column_count):
    keep_mask = live_row.astype(key_grads.dtype)
    weighted = (key_grads * keep_mask[:, None, None]).reshape(-1, key_grads.shape[2])
    columns = inputs.reshape(-1, column_count)
    return lax.dot_general(
        weighted, columns, (((0,), (0,)), ((), ())), preferred_element_type=jnp.float32
    )


def butterfly_sum(value, axes):
    for axis in axes:
        size = lax.axis_size(axis)
        if size & (size - 1):
            value = lax.psum(value, axis)
            continue
        bit = 1
        while bit < size:
            pairs = [(i, i ^ bit) for i in range(size)]
            value = value + lax.ppermute(value, axis, pairs)
            bit *= 2
    return value


def bit_orders(size):
    bits = list(range(size.bit_length() - 1))
    return bits, bits[1:2] + bits[:1] + bits[2:], bits[:1] + bits[2:3] + bits[1:2] + bits[3:]


def halving_scatter(partial, axis, order):
    size = lax.axis_size(axis)
    index = lax.axis_index(axis)
    width = partial.shape[1] // size
    held = list(range(size))
    blocks = partial
    for bit in order:
        mine = (index >> bit) & 1
        low = [k for k, block in enumerate(held) if not (block >> bit) & 1]
        high = [k for k, block in enumerate(held) if (block >> bit) & 1]
        low_part = jnp.concatenate([blocks[:, k * width:(k + 1) * width] for k in low], axis=1)
        high_part = jnp.concatenate([blocks[:, k * width:(k + 1) * width] for k in high], axis=1)
        keep = jnp.where(mine == 1, high_part, low_part)
        send = jnp.where(mine == 1, low_part, high_part)
        pairs = [(i, i ^ (1 << bit)) for i in range(size)]
        blocks = keep + lax.ppermute(send, axis, pairs)
        held = [held[k] & ~(1 << bit) for k in low]
    return blocks


def doubling_gather(part, axis, order):
    size = lax.axis_size(axis)
    levels = size.bit_length() - 1
    index = lax.axis_index(axis)
    placed = []
    current = part
    for bit in order:
        mine = (index >> bit) & 1
        pairs = [(i, i ^ (1 << bit)) for i in range(size)]
        other = lax.ppermute(current, axis, pairs)
        low = jnp.where(mine == 1, other, current)
        high = jnp.where(mine == 1, current, other)
        current = jnp.stack([low, high], axis=0)
        placed.insert(0, bit)
    perm = [placed.index(bit) for bit in range(levels - 1, -1, -1)]
    current = jnp.transpose(current, perm + list(range(levels, current.ndim)))
    return current.reshape((-1,) + part.shape[1:])


def scatter_rows(partial_t, axis, parts=4):
    size = lax.axis_size(axis)
    cols = partial_t.shape[0]
    if size & (size - 1) or size == 1 or cols % (8 * parts):
        return lax.psum_scatter(partial_t, axis, scatter_dimension=1, tiled=True)
    orders = bit_orders(size)
    width = cols // parts
    return jnp.concatenate(
        [
            halving_scatter(partial_t[k * width:(k + 1) * width], axis, orders[(0, 1, 2, 1)[k % 4]])
            for k in range(parts)
        ],
        axis=0,
    )


def gather_rows(part, axis):
    size = lax.axis_size(axis)
    cols = part.shape[1]
    if size & (size - 1) or size == 1 or cols % 2:
        return lax.all_gather(part, axis, axis=0, tiled=True)
    first, second = bit_orders(size)[:2]
    half = cols // 2
    return jnp.concatenate(
        [
            doubling_gather(part[:, :half], axis, first[::-1]),
            doubling_gather(part[:, half:], axis, bit_orders(size)[2]),
        ],
        axis=1,
    )


def local(normed_input, key_grad, live_slots, master, first_moment, second_moment):
    inputs = normed_input[0]
    key_grads = key_grad[0]
    live_row = live_slots[0]
    live_count = jnp.sum(live_row)
    features = inputs.shape[2]
    summed = scatter_rows(slot_term(inputs, key_grads, live_row, features), "dp")
    tokens_total = (live_count * (inputs.shape[1] * lax.axis_size("dp"))).astype(jnp.float32)
    grad_shard = summed / tokens_total
    squares = butterfly_sum(jnp.sum(grad_shard * grad_shard), ("pipe", "tensor", "dp"))
    clip_factor = jnp.minimum(1.0, CLIP_NORM / jnp.sqrt(squares))
    clipped = clip_factor * grad_shard
    moment1 = MOMENT_DECAY * first_moment[0].T + (1.0 - MOMENT_DECAY) * clipped
    moment2 = SQUARE_DECAY * second_moment[0].T + (1.0 - SQUARE_DECAY) * clipped * clipped
    update = (
        moment1 / FIRST_CORRECTION / (jnp.sqrt(moment2 / SECOND_CORRECTION) + EPSILON)
        + WEIGHT_DECAY * master[0].T
    )
    return gather_rows(update.astype(jnp.bfloat16).T, "dp")[None]


def solution(mesh):
    in_specs = (
        P("pipe", None, "dp", None),
        P("pipe", None, "dp", "tensor"),
        P("pipe", None),
        P("pipe", "dp", "tensor"),
        P("pipe", "dp", "tensor"),
        P("pipe", "dp", "tensor"),
    )
    out_specs = P("pipe", None, "tensor")
    return jax.shard_map(local, mesh=mesh, in_specs=in_specs, out_specs=out_specs, check_vma=False)
```

```python
import jax
import jax.numpy as jnp
from jax import lax
from jax.sharding import PartitionSpec as P

MOMENT_DECAY = 0.9
SQUARE_DECAY = 0.95
FIRST_CORRECTION = 1.0 - 0.9**20
SECOND_CORRECTION = 1.0 - 0.95**20
WEIGHT_DECAY = 0.1
CLIP_NORM = 1.0
EPSILON = 1e-08


def slot_term(inputs, key_grads, live_row, column_count):
    keep_mask = live_row.astype(key_grads.dtype)
    weighted = (key_grads * keep_mask[:, None, None]).reshape(-1, key_grads.shape[2])
    columns = inputs.reshape(-1, column_count)
    return lax.dot_general(
        weighted, columns, (((0,), (0,)), ((), ())), preferred_element_type=jnp.float32
    )


def butterfly_sum(value, axes):
    for axis in axes:
        size = lax.axis_size(axis)
        if size & (size - 1):
            value = lax.psum(value, axis)
            continue
        bit = 1
        while bit < size:
            pairs = [(i, i ^ bit) for i in range(size)]
            value = value + lax.ppermute(value, axis, pairs)
            bit *= 2
    return value


def bit_orders(size):
    bits = list(range(size.bit_length() - 1))
    return bits, bits[1:2] + bits[:1] + bits[2:], bits[:1] + bits[2:3] + bits[1:2] + bits[3:]


def halving_scatter(partial, axis, order):
    size = lax.axis_size(axis)
    index = lax.axis_index(axis)
    width = partial.shape[1] // size
    held = list(range(size))
    blocks = partial
    for bit in order:
        mine = (index >> bit) & 1
        low = [k for k, block in enumerate(held) if not (block >> bit) & 1]
        high = [k for k, block in enumerate(held) if (block >> bit) & 1]
        low_part = jnp.concatenate([blocks[:, k * width:(k + 1) * width] for k in low], axis=1)
        high_part = jnp.concatenate([blocks[:, k * width:(k + 1) * width] for k in high], axis=1)
        keep = jnp.where(mine == 1, high_part, low_part)
        send = jnp.where(mine == 1, low_part, high_part)
        pairs = [(i, i ^ (1 << bit)) for i in range(size)]
        blocks = keep + lax.ppermute(send, axis, pairs)
        held = [held[k] & ~(1 << bit) for k in low]
    return blocks


def doubling_gather(part, axis, order):
    size = lax.axis_size(axis)
    index = lax.axis_index(axis)
    height = part.shape[0]
    held = [0]
    blocks = part
    for bit in order:
        mine = (index >> bit) & 1
        pairs = [(i, i ^ (1 << bit)) for i in range(size)]
        other = lax.ppermute(blocks, axis, pairs)
        low = jnp.where(mine == 1, other, blocks)
        high = jnp.where(mine == 1, blocks, other)
        merged = sorted([(block, 0, k) for k, block in enumerate(held)] + [(block | (1 << bit), 1, k) for k, block in enumerate(held)])
        blocks = jnp.concatenate(
            [(high if side else low)[k * height:(k + 1) * height] for _, side, k in merged], axis=0
        )
        held = [block for block, _, _ in merged]
    return blocks


def scatter_rows(partial_t, axis, parts=4):
    size = lax.axis_size(axis)
    cols = partial_t.shape[0]
    if size & (size - 1) or size == 1 or cols % (8 * parts):
        return lax.psum_scatter(partial_t, axis, scatter_dimension=1, tiled=True)
    orders = bit_orders(size)
    width = cols // parts
    return jnp.concatenate(
        [
            halving_scatter(partial_t[k * width:(k + 1) * width], axis, orders[(0, 1, 2, 1)[k % 4]])
            for k in range(parts)
        ],
        axis=0,
    )


def gather_rows(part, axis):
    size = lax.axis_size(axis)
    cols = part.shape[1]
    if size & (size - 1) or size == 1 or cols % 2:
        return lax.all_gather(part, axis, axis=0, tiled=True)
    first, second = bit_orders(size)[:2]
    half = cols // 2
    return jnp.concatenate(
        [
            doubling_gather(part[:, :half], axis, first[::-1]),
            doubling_gather(part[:, half:], axis, bit_orders(size)[2]),
        ],
        axis=1,
    )


def local(normed_input, key_grad, live_slots, master, first_moment, second_moment):
    inputs = normed_input[0]
    key_grads = key_grad[0]
    live_row = live_slots[0]
    live_count = jnp.sum(live_row)
    features = inputs.shape[2]
    summed = scatter_rows(slot_term(inputs, key_grads, live_row, features), "dp")
    tokens_total = (live_count * (inputs.shape[1] * lax.axis_size("dp"))).astype(jnp.float32)
    grad_shard = summed / tokens_total
    squares = butterfly_sum(jnp.sum(grad_shard * grad_shard), ("pipe", "tensor", "dp"))
    clip_factor = jnp.minimum(1.0, CLIP_NORM / jnp.sqrt(squares))
    clipped = clip_factor * grad_shard
    moment1 = MOMENT_DECAY * first_moment[0].T + (1.0 - MOMENT_DECAY) * clipped
    moment2 = SQUARE_DECAY * second_moment[0].T + (1.0 - SQUARE_DECAY) * clipped * clipped
    update = (
        moment1 / FIRST_CORRECTION / (jnp.sqrt(moment2 / SECOND_CORRECTION) + EPSILON)
        + WEIGHT_DECAY * master[0].T
    )
    return gather_rows(update.astype(jnp.bfloat16).T, "dp")[None]


def solution(mesh):
    in_specs = (
        P("pipe", None, "dp", None),
        P("pipe", None, "dp", "tensor"),
        P("pipe", None),
        P("pipe", "dp", "tensor"),
        P("pipe", "dp", "tensor"),
        P("pipe", "dp", "tensor"),
    )
    out_specs = P("pipe", None, "tensor")
    return jax.shard_map(local, mesh=mesh, in_specs=in_specs, out_specs=out_specs, check_vma=False)
```

```python
import jax
import jax.numpy as jnp
from jax import lax
from jax.sharding import PartitionSpec as P

MOMENT_DECAY = 0.9
SQUARE_DECAY = 0.95
FIRST_CORRECTION = 1.0 - 0.9**20
SECOND_CORRECTION = 1.0 - 0.95**20
WEIGHT_DECAY = 0.1
CLIP_NORM = 1.0
EPSILON = 1e-08


def slot_term(inputs, key_grads, live_row, column_count):
    live = live_row[:, None, None] == 1
    weighted = jnp.where(live, key_grads, jnp.zeros_like(key_grads)).reshape(-1, key_grads.shape[2])
    columns = inputs.reshape(-1, column_count)
    return lax.dot_general(
        weighted, columns, (((0,), (0,)), ((), ())), preferred_element_type=jnp.float32
    )


def butterfly_sum(value, axes):
    for axis in axes:
        size = lax.axis_size(axis)
        if size & (size - 1):
            value = lax.psum(value, axis)
            continue
        bit = 1
        while bit < size:
            pairs = [(i, i ^ bit) for i in range(size)]
            value = value + lax.ppermute(value, axis, pairs)
            bit *= 2
    return value


def bit_orders(size):
    bits = list(range(size.bit_length() - 1))
    return bits, bits[1:2] + bits[:1] + bits[2:], bits[:1] + bits[2:3] + bits[1:2] + bits[3:]


def halving_scatter(partial, axis, order):
    size = lax.axis_size(axis)
    index = lax.axis_index(axis)
    width = partial.shape[1] // size
    held = list(range(size))
    blocks = partial
    for bit in order:
        mine = (index >> bit) & 1
        low = [k for k, block in enumerate(held) if not (block >> bit) & 1]
        high = [k for k, block in enumerate(held) if (block >> bit) & 1]
        low_part = jnp.concatenate([blocks[:, k * width:(k + 1) * width] for k in low], axis=1)
        high_part = jnp.concatenate([blocks[:, k * width:(k + 1) * width] for k in high], axis=1)
        keep = jnp.where(mine == 1, high_part, low_part)
        send = jnp.where(mine == 1, low_part, high_part)
        pairs = [(i, i ^ (1 << bit)) for i in range(size)]
        blocks = keep + lax.ppermute(send, axis, pairs)
        held = [held[k] & ~(1 << bit) for k in low]
    return blocks


def doubling_gather(part, axis, order):
    size = lax.axis_size(axis)
    levels = size.bit_length() - 1
    index = lax.axis_index(axis)
    placed = []
    current = part
    for bit in order:
        mine = (index >> bit) & 1
        pairs = [(i, i ^ (1 << bit)) for i in range(size)]
        other = lax.ppermute(current, axis, pairs)
        low = jnp.where(mine == 1, other, current)
        high = jnp.where(mine == 1, current, other)
        current = jnp.stack([low, high], axis=0)
        placed.insert(0, bit)
    perm = [placed.index(bit) for bit in range(levels - 1, -1, -1)]
    current = jnp.transpose(current, perm + list(range(levels, current.ndim)))
    return current.reshape((-1,) + part.shape[1:])


def scatter_rows(partial_t, axis, parts=4):
    size = lax.axis_size(axis)
    cols = partial_t.shape[0]
    if size & (size - 1) or size == 1 or cols % (8 * parts):
        return lax.psum_scatter(partial_t, axis, scatter_dimension=1, tiled=True)
    orders = bit_orders(size)
    width = cols // parts
    return jnp.concatenate(
        [
            halving_scatter(partial_t[k * width:(k + 1) * width], axis, orders[(0, 1, 2, 1)[k % 4]])
            for k in range(parts)
        ],
        axis=0,
    )


def gather_rows(part, axis):
    size = lax.axis_size(axis)
    cols = part.shape[1]
    if size & (size - 1) or size == 1 or cols % 2:
        return lax.all_gather(part, axis, axis=0, tiled=True)
    first, second = bit_orders(size)[:2]
    half = cols // 2
    return jnp.concatenate(
        [
            doubling_gather(part[:, :half], axis, first[::-1]),
            doubling_gather(part[:, half:], axis, bit_orders(size)[2]),
        ],
        axis=1,
    )


def local(normed_input, key_grad, live_slots, master, first_moment, second_moment):
    inputs = normed_input[0]
    key_grads = key_grad[0]
    live_row = live_slots[0]
    live_count = jnp.sum(live_row)
    features = inputs.shape[2]
    summed = scatter_rows(slot_term(inputs, key_grads, live_row, features), "dp")
    tokens_total = (live_count * (inputs.shape[1] * lax.axis_size("dp"))).astype(jnp.float32)
    grad_shard = summed / tokens_total
    squares = butterfly_sum(jnp.sum(grad_shard * grad_shard), ("pipe", "tensor", "dp"))
    clip_factor = jnp.minimum(1.0, CLIP_NORM / jnp.sqrt(squares))
    clipped = clip_factor * grad_shard
    moment1 = MOMENT_DECAY * first_moment[0].T + (1.0 - MOMENT_DECAY) * clipped
    moment2 = SQUARE_DECAY * second_moment[0].T + (1.0 - SQUARE_DECAY) * clipped * clipped
    update = (
        moment1 / FIRST_CORRECTION / (jnp.sqrt(moment2 / SECOND_CORRECTION) + EPSILON)
        + WEIGHT_DECAY * master[0].T
    )
    return gather_rows(update.astype(jnp.bfloat16).T, "dp")[None]


def solution(mesh):
    in_specs = (
        P("pipe", None, "dp", None),
        P("pipe", None, "dp", "tensor"),
        P("pipe", None),
        P("pipe", "dp", "tensor"),
        P("pipe", "dp", "tensor"),
        P("pipe", "dp", "tensor"),
    )
    out_specs = P("pipe", None, "tensor")
    return jax.shard_map(local, mesh=mesh, in_specs=in_specs, out_specs=out_specs, check_vma=False)
```

```python
import jax
import jax.numpy as jnp
from jax import lax
from jax.sharding import PartitionSpec as P

MOMENT_DECAY = 0.9
SQUARE_DECAY = 0.95
FIRST_CORRECTION = 1.0 - 0.9**20
SECOND_CORRECTION = 1.0 - 0.95**20
WEIGHT_DECAY = 0.1
CLIP_NORM = 1.0
EPSILON = 1e-08


def slot_term(inputs, key_grads, live_row, column_count):
    live = live_row[:, None, None] == 1
    weighted = jnp.where(live, key_grads, jnp.zeros_like(key_grads)).reshape(-1, key_grads.shape[2])
    columns = inputs.reshape(-1, column_count)
    return lax.dot_general(
        weighted, columns, (((0,), (0,)), ((), ())), preferred_element_type=jnp.float32
    )


def butterfly_sum(value, axes):
    for axis in axes:
        size = lax.axis_size(axis)
        if size & (size - 1):
            value = lax.psum(value, axis)
            continue
        bit = 1
        while bit < size:
            pairs = [(i, i ^ bit) for i in range(size)]
            value = value + lax.ppermute(value, axis, pairs)
            bit *= 2
    return value


def bit_orders(size):
    bits = list(range(size.bit_length() - 1))
    return bits, bits[1:2] + bits[:1] + bits[2:], bits[:1] + bits[2:3] + bits[1:2] + bits[3:]


def halving_scatter(partial, axis, order):
    size = lax.axis_size(axis)
    index = lax.axis_index(axis)
    width = partial.shape[1] // size
    held = list(range(size))
    blocks = partial
    for bit in order:
        mine = (index >> bit) & 1
        low = [k for k, block in enumerate(held) if not (block >> bit) & 1]
        high = [k for k, block in enumerate(held) if (block >> bit) & 1]
        low_part = jnp.concatenate([blocks[:, k * width:(k + 1) * width] for k in low], axis=1)
        high_part = jnp.concatenate([blocks[:, k * width:(k + 1) * width] for k in high], axis=1)
        keep = jnp.where(mine == 1, high_part, low_part)
        send = jnp.where(mine == 1, low_part, high_part)
        pairs = [(i, i ^ (1 << bit)) for i in range(size)]
        blocks = keep + lax.ppermute(send, axis, pairs)
        held = [held[k] & ~(1 << bit) for k in low]
    return blocks


def doubling_gather(part, axis, order):
    size = lax.axis_size(axis)
    levels = size.bit_length() - 1
    index = lax.axis_index(axis)
    placed = []
    current = part
    for bit in order:
        mine = (index >> bit) & 1
        pairs = [(i, i ^ (1 << bit)) for i in range(size)]
        other = lax.ppermute(current, axis, pairs)
        low = jnp.where(mine == 1, other, current)
        high = jnp.where(mine == 1, current, other)
        current = jnp.stack([low, high], axis=0)
        placed.insert(0, bit)
    perm = [placed.index(bit) for bit in range(levels - 1, -1, -1)]
    current = jnp.transpose(current, perm + list(range(levels, current.ndim)))
    return current.reshape((-1,) + part.shape[1:])


def scatter_rows(partial_t, axis, parts=4):
    size = lax.axis_size(axis)
    cols = partial_t.shape[0]
    if size & (size - 1) or size == 1 or cols % (8 * parts):
        return lax.psum_scatter(partial_t, axis, scatter_dimension=1, tiled=True)
    orders = bit_orders(size)
    width = cols // parts
    return jnp.concatenate(
        [
            halving_scatter(partial_t[k * width:(k + 1) * width], axis, orders[(0, 1, 2, 1)[k % 4]])
            for k in range(parts)
        ],
        axis=0,
    )


def gather_rows(part, axis):
    size = lax.axis_size(axis)
    cols = part.shape[1]
    if size & (size - 1) or size == 1 or cols % 2:
        return lax.all_gather(part, axis, axis=0, tiled=True)
    first, second = bit_orders(size)[:2]
    half = cols // 2
    return jnp.concatenate(
        [
            doubling_gather(part[:, :half], axis, first[::-1]),
            doubling_gather(part[:, half:], axis, bit_orders(size)[2]),
        ],
        axis=1,
    )


def local(normed_input, key_grad, live_slots, master, first_moment, second_moment):
    inputs = normed_input[0]
    key_grads = key_grad[0]
    live_row = live_slots[0]
    live_count = jnp.sum(live_row)
    features = inputs.shape[2]
    summed = scatter_rows(slot_term(inputs, key_grads, live_row, features), "dp")
    tokens_total = (live_count * (inputs.shape[1] * lax.axis_size("dp"))).astype(jnp.float32)
    grad_shard = summed / tokens_total
    squares = butterfly_sum(jnp.sum(grad_shard * grad_shard), ("dp", "tensor", "pipe"))
    clip_factor = jnp.minimum(1.0, CLIP_NORM / jnp.sqrt(squares))
    clipped = clip_factor * grad_shard
    moment1 = MOMENT_DECAY * first_moment[0].T + (1.0 - MOMENT_DECAY) * clipped
    moment2 = SQUARE_DECAY * second_moment[0].T + (1.0 - SQUARE_DECAY) * clipped * clipped
    update = (
        moment1 / FIRST_CORRECTION / (jnp.sqrt(moment2 / SECOND_CORRECTION) + EPSILON)
        + WEIGHT_DECAY * master[0].T
    )
    return gather_rows(update.astype(jnp.bfloat16).T, "dp")[None]


def solution(mesh):
    in_specs = (
        P("pipe", None, "dp", None),
        P("pipe", None, "dp", "tensor"),
        P("pipe", None),
        P("pipe", "dp", "tensor"),
        P("pipe", "dp", "tensor"),
        P("pipe", "dp", "tensor"),
    )
    out_specs = P("pipe", None, "tensor")
    return jax.shard_map(local, mesh=mesh, in_specs=in_specs, out_specs=out_specs, check_vma=False)
```

```python
import jax
import jax.numpy as jnp
from jax import lax
from jax.sharding import PartitionSpec as P

MOMENT_DECAY = 0.9
SQUARE_DECAY = 0.95
FIRST_CORRECTION = 1.0 - 0.9**20
SECOND_CORRECTION = 1.0 - 0.95**20
WEIGHT_DECAY = 0.1
CLIP_NORM = 1.0
EPSILON = 1e-08


def slot_term(inputs, key_grads, live_row, column_count):
    live = live_row[:, None, None] == 1
    weighted = jnp.where(live, key_grads, jnp.zeros_like(key_grads)).reshape(-1, key_grads.shape[2])
    columns = inputs.reshape(-1, column_count)
    return lax.dot_general(
        weighted, columns, (((0,), (0,)), ((), ())), preferred_element_type=jnp.float32
    )


def butterfly_sum(value, axes):
    for axis in axes:
        size = lax.axis_size(axis)
        if size & (size - 1):
            value = lax.psum(value, axis)
            continue
        bit = 1
        while bit < size:
            pairs = [(i, i ^ bit) for i in range(size)]
            value = value + lax.ppermute(value, axis, pairs)
            bit *= 2
    return value


def bit_orders(size):
    bits = list(range(size.bit_length() - 1))
    return bits, bits[1:2] + bits[:1] + bits[2:], bits[:1] + bits[2:3] + bits[1:2] + bits[3:]


def halving_scatter(partial, axis, order):
    size = lax.axis_size(axis)
    index = lax.axis_index(axis)
    width = partial.shape[1] // size
    held = list(range(size))
    blocks = partial
    for bit in order:
        mine = (index >> bit) & 1
        low = [k for k, block in enumerate(held) if not (block >> bit) & 1]
        high = [k for k, block in enumerate(held) if (block >> bit) & 1]
        low_part = jnp.concatenate([blocks[:, k * width:(k + 1) * width] for k in low], axis=1)
        high_part = jnp.concatenate([blocks[:, k * width:(k + 1) * width] for k in high], axis=1)
        keep = jnp.where(mine == 1, high_part, low_part)
        send = jnp.where(mine == 1, low_part, high_part)
        pairs = [(i, i ^ (1 << bit)) for i in range(size)]
        blocks = keep + lax.ppermute(send, axis, pairs)
        held = [held[k] & ~(1 << bit) for k in low]
    return blocks


def doubling_gather(part, axis, order):
    size = lax.axis_size(axis)
    levels = size.bit_length() - 1
    index = lax.axis_index(axis)
    placed = []
    current = part
    for bit in order:
        mine = (index >> bit) & 1
        pairs = [(i, i ^ (1 << bit)) for i in range(size)]
        other = lax.ppermute(current, axis, pairs)
        low = jnp.where(mine == 1, other, current)
        high = jnp.where(mine == 1, current, other)
        current = jnp.stack([low, high], axis=0)
        placed.insert(0, bit)
    perm = [placed.index(bit) for bit in range(levels - 1, -1, -1)]
    current = jnp.transpose(current, perm + list(range(levels, current.ndim)))
    return current.reshape((-1,) + part.shape[1:])


def scatter_rows(partial_t, axis, parts=4):
    size = lax.axis_size(axis)
    cols = partial_t.shape[0]
    if size & (size - 1) or size == 1 or cols % (8 * parts):
        return lax.psum_scatter(partial_t, axis, scatter_dimension=1, tiled=True)
    orders = bit_orders(size)
    width = cols // parts
    return jnp.concatenate(
        [
            halving_scatter(partial_t[k * width:(k + 1) * width], axis, orders[(0, 1, 2, 1)[k % 4]])
            for k in range(parts)
        ],
        axis=0,
    )


def gather_rows(part, axis):
    size = lax.axis_size(axis)
    cols = part.shape[1]
    if size & (size - 1) or size == 1 or cols % 2:
        return lax.all_gather(part, axis, axis=0, tiled=True)
    first, second = bit_orders(size)[:2]
    half = cols // 2
    return jnp.concatenate(
        [
            doubling_gather(part[:, :half], axis, first[::-1]),
            doubling_gather(part[:, half:], axis, bit_orders(size)[2]),
        ],
        axis=1,
    )


def local(normed_input, key_grad, live_slots, master, first_moment, second_moment):
    inputs = normed_input[0]
    key_grads = key_grad[0]
    live_row = live_slots[0]
    live_count = jnp.sum(live_row)
    features = inputs.shape[2]
    summed = scatter_rows(slot_term(inputs, key_grads, live_row, features), "dp")
    tokens_total = (live_count * (inputs.shape[1] * lax.axis_size("dp"))).astype(jnp.float32)
    grad_shard = summed / tokens_total
    squares = butterfly_sum(jnp.sum(grad_shard * grad_shard), ("tensor", "pipe", "dp"))
    clip_factor = jnp.minimum(1.0, CLIP_NORM / jnp.sqrt(squares))
    clipped = clip_factor * grad_shard
    moment1 = MOMENT_DECAY * first_moment[0].T + (1.0 - MOMENT_DECAY) * clipped
    moment2 = SQUARE_DECAY * second_moment[0].T + (1.0 - SQUARE_DECAY) * clipped * clipped
    update = (
        moment1 / FIRST_CORRECTION / (jnp.sqrt(moment2 / SECOND_CORRECTION) + EPSILON)
        + WEIGHT_DECAY * master[0].T
    )
    return gather_rows(update.astype(jnp.bfloat16).T, "dp")[None]


def solution(mesh):
    in_specs = (
        P("pipe", None, "dp", None),
        P("pipe", None, "dp", "tensor"),
        P("pipe", None),
        P("pipe", "dp", "tensor"),
        P("pipe", "dp", "tensor"),
        P("pipe", "dp", "tensor"),
    )
    out_specs = P("pipe", None, "tensor")
    return jax.shard_map(local, mesh=mesh, in_specs=in_specs, out_specs=out_specs, check_vma=False)
```

```python
import jax
import jax.numpy as jnp
from jax import lax
from jax.sharding import PartitionSpec as P

MOMENT_DECAY = 0.9
SQUARE_DECAY = 0.95
FIRST_CORRECTION = 1.0 - 0.9**20
SECOND_CORRECTION = 1.0 - 0.95**20
WEIGHT_DECAY = 0.1
CLIP_NORM = 1.0
EPSILON = 1e-08


def slot_term(inputs, key_grads, live_row, column_count):
    live = live_row[:, None, None] == 1
    weighted = jnp.where(live, key_grads, jnp.zeros_like(key_grads)).reshape(-1, key_grads.shape[2])
    columns = inputs.reshape(-1, column_count)
    return lax.dot_general(
        weighted, columns, (((0,), (0,)), ((), ())), preferred_element_type=jnp.float32
    )


def butterfly_sum(value, axes):
    for axis in axes:
        size = lax.axis_size(axis)
        if size & (size - 1):
            value = lax.psum(value, axis)
            continue
        bit = 1
        while bit < size:
            pairs = [(i, i ^ bit) for i in range(size)]
            value = value + lax.ppermute(value, axis, pairs)
            bit *= 2
    return value


def bit_orders(size):
    bits = list(range(size.bit_length() - 1))
    return bits, bits[1:2] + bits[:1] + bits[2:], bits[:1] + bits[2:3] + bits[1:2] + bits[3:]


def halving_scatter(partial, axis, order):
    size = lax.axis_size(axis)
    index = lax.axis_index(axis)
    width = partial.shape[1] // size
    held = list(range(size))
    blocks = partial
    for bit in order:
        mine = (index >> bit) & 1
        low = [k for k, block in enumerate(held) if not (block >> bit) & 1]
        high = [k for k, block in enumerate(held) if (block >> bit) & 1]
        low_part = jnp.concatenate([blocks[:, k * width:(k + 1) * width] for k in low], axis=1)
        high_part = jnp.concatenate([blocks[:, k * width:(k + 1) * width] for k in high], axis=1)
        keep = jnp.where(mine == 1, high_part, low_part)
        send = jnp.where(mine == 1, low_part, high_part)
        pairs = [(i, i ^ (1 << bit)) for i in range(size)]
        blocks = keep + lax.ppermute(send, axis, pairs)
        held = [held[k] & ~(1 << bit) for k in low]
    return blocks


def doubling_gather(part, axis, order):
    size = lax.axis_size(axis)
    levels = size.bit_length() - 1
    index = lax.axis_index(axis)
    placed = []
    current = part
    for bit in order:
        mine = (index >> bit) & 1
        pairs = [(i, i ^ (1 << bit)) for i in range(size)]
        other = lax.ppermute(current, axis, pairs)
        low = jnp.where(mine == 1, other, current)
        high = jnp.where(mine == 1, current, other)
        current = jnp.stack([low, high], axis=0)
        placed.insert(0, bit)
    perm = [placed.index(bit) for bit in range(levels - 1, -1, -1)]
    current = jnp.transpose(current, perm + list(range(levels, current.ndim)))
    return current.reshape((-1,) + part.shape[1:])


def scatter_rows(partial_t, axis, parts=4):
    size = lax.axis_size(axis)
    cols = partial_t.shape[0]
    if size & (size - 1) or size == 1 or cols % (8 * parts):
        return lax.psum_scatter(partial_t, axis, scatter_dimension=1, tiled=True)
    orders = bit_orders(size)
    width = cols // parts
    return jnp.concatenate(
        [
            halving_scatter(partial_t[k * width:(k + 1) * width], axis, orders[(0, 1, 2, 1)[k % 4]])
            for k in range(parts)
        ],
        axis=0,
    )


def gather_rows(part, axis):
    size = lax.axis_size(axis)
    cols = part.shape[1]
    if size & (size - 1) or size == 1 or cols % 2:
        return lax.all_gather(part, axis, axis=0, tiled=True)
    first, second = bit_orders(size)[:2]
    half = cols // 2
    return jnp.concatenate(
        [
            doubling_gather(part[:, :half], axis, first[::-1]),
            doubling_gather(part[:, half:], axis, bit_orders(size)[2]),
        ],
        axis=1,
    )


def local(normed_input, key_grad, live_slots, master, first_moment, second_moment):
    inputs = normed_input[0]
    key_grads = key_grad[0]
    live_row = live_slots[0]
    live_count = jnp.sum(live_row)
    features = inputs.shape[2]
    summed = scatter_rows(slot_term(inputs, key_grads, live_row, features), "dp")
    tokens_total = (live_count * (inputs.shape[1] * lax.axis_size("dp"))).astype(jnp.float32)
    grad_shard = summed / tokens_total
    squares = butterfly_sum(jnp.sum(grad_shard * grad_shard), ("tensor", "dp", "pipe"))
    clip_factor = jnp.minimum(1.0, CLIP_NORM / jnp.sqrt(squares))
    clipped = clip_factor * grad_shard
    moment1 = MOMENT_DECAY * first_moment[0].T + (1.0 - MOMENT_DECAY) * clipped
    moment2 = SQUARE_DECAY * second_moment[0].T + (1.0 - SQUARE_DECAY) * clipped * clipped
    update = (
        moment1 / FIRST_CORRECTION / (jnp.sqrt(moment2 / SECOND_CORRECTION) + EPSILON)
        + WEIGHT_DECAY * master[0].T
    )
    return gather_rows(update.astype(jnp.bfloat16).T, "dp")[None]


def solution(mesh):
    in_specs = (
        P("pipe", None, "dp", None),
        P("pipe", None, "dp", "tensor"),
        P("pipe", None),
        P("pipe", "dp", "tensor"),
        P("pipe", "dp", "tensor"),
        P("pipe", "dp", "tensor"),
    )
    out_specs = P("pipe", None, "tensor")
    return jax.shard_map(local, mesh=mesh, in_specs=in_specs, out_specs=out_specs, check_vma=False)
```

```python
import jax
import jax.numpy as jnp
from jax import lax
from jax.sharding import PartitionSpec as P

MOMENT_DECAY = 0.9
SQUARE_DECAY = 0.95
FIRST_CORRECTION = 1.0 - 0.9**20
SECOND_CORRECTION = 1.0 - 0.95**20
WEIGHT_DECAY = 0.1
CLIP_NORM = 1.0
EPSILON = 1e-08


def slot_term(inputs, key_grads, live_row, column_count):
    live = live_row[:, None, None] == 1
    weighted = jnp.where(live, key_grads, jnp.zeros_like(key_grads)).reshape(-1, key_grads.shape[2])
    columns = inputs.reshape(-1, column_count)
    return lax.dot_general(
        weighted, columns, (((0,), (0,)), ((), ())), preferred_element_type=jnp.float32
    )


def butterfly_sum(value, axes):
    for axis in axes:
        size = lax.axis_size(axis)
        if size & (size - 1):
            value = lax.psum(value, axis)
            continue
        bit = size // 2
        while bit >= 1:
            pairs = [(i, i ^ bit) for i in range(size)]
            value = value + lax.ppermute(value, axis, pairs)
            bit //= 2
    return value


def bit_orders(size):
    bits = list(range(size.bit_length() - 1))
    return bits, bits[1:2] + bits[:1] + bits[2:], bits[:1] + bits[2:3] + bits[1:2] + bits[3:]


def halving_scatter(partial, axis, order):
    size = lax.axis_size(axis)
    index = lax.axis_index(axis)
    width = partial.shape[1] // size
    held = list(range(size))
    blocks = partial
    for bit in order:
        mine = (index >> bit) & 1
        low = [k for k, block in enumerate(held) if not (block >> bit) & 1]
        high = [k for k, block in enumerate(held) if (block >> bit) & 1]
        low_part = jnp.concatenate([blocks[:, k * width:(k + 1) * width] for k in low], axis=1)
        high_part = jnp.concatenate([blocks[:, k * width:(k + 1) * width] for k in high], axis=1)
        keep = jnp.where(mine == 1, high_part, low_part)
        send = jnp.where(mine == 1, low_part, high_part)
        pairs = [(i, i ^ (1 << bit)) for i in range(size)]
        blocks = keep + lax.ppermute(send, axis, pairs)
        held = [held[k] & ~(1 << bit) for k in low]
    return blocks


def doubling_gather(part, axis, order):
    size = lax.axis_size(axis)
    levels = size.bit_length() - 1
    index = lax.axis_index(axis)
    placed = []
    current = part
    for bit in order:
        mine = (index >> bit) & 1
        pairs = [(i, i ^ (1 << bit)) for i in range(size)]
        other = lax.ppermute(current, axis, pairs)
        low = jnp.where(mine == 1, other, current)
        high = jnp.where(mine == 1, current, other)
        current = jnp.stack([low, high], axis=0)
        placed.insert(0, bit)
    perm = [placed.index(bit) for bit in range(levels - 1, -1, -1)]
    current = jnp.transpose(current, perm + list(range(levels, current.ndim)))
    return current.reshape((-1,) + part.shape[1:])


def scatter_rows(partial_t, axis, parts=4):
    size = lax.axis_size(axis)
    cols = partial_t.shape[0]
    if size & (size - 1) or size == 1 or cols % (8 * parts):
        return lax.psum_scatter(partial_t, axis, scatter_dimension=1, tiled=True)
    orders = bit_orders(size)
    width = cols // parts
    return jnp.concatenate(
        [
            halving_scatter(partial_t[k * width:(k + 1) * width], axis, orders[(0, 1, 2, 1)[k % 4]])
            for k in range(parts)
        ],
        axis=0,
    )


def gather_rows(part, axis):
    size = lax.axis_size(axis)
    cols = part.shape[1]
    if size & (size - 1) or size == 1 or cols % 2:
        return lax.all_gather(part, axis, axis=0, tiled=True)
    first, second = bit_orders(size)[:2]
    half = cols // 2
    return jnp.concatenate(
        [
            doubling_gather(part[:, :half], axis, first[::-1]),
            doubling_gather(part[:, half:], axis, bit_orders(size)[2]),
        ],
        axis=1,
    )


def local(normed_input, key_grad, live_slots, master, first_moment, second_moment):
    inputs = normed_input[0]
    key_grads = key_grad[0]
    live_row = live_slots[0]
    live_count = jnp.sum(live_row)
    features = inputs.shape[2]
    summed = scatter_rows(slot_term(inputs, key_grads, live_row, features), "dp")
    tokens_total = (live_count * (inputs.shape[1] * lax.axis_size("dp"))).astype(jnp.float32)
    grad_shard = summed / tokens_total
    squares = butterfly_sum(jnp.sum(grad_shard * grad_shard), ("tensor", "pipe", "dp"))
    clip_factor = jnp.minimum(1.0, CLIP_NORM / jnp.sqrt(squares))
    clipped = clip_factor * grad_shard
    moment1 = MOMENT_DECAY * first_moment[0].T + (1.0 - MOMENT_DECAY) * clipped
    moment2 = SQUARE_DECAY * second_moment[0].T + (1.0 - SQUARE_DECAY) * clipped * clipped
    update = (
        moment1 / FIRST_CORRECTION / (jnp.sqrt(moment2 / SECOND_CORRECTION) + EPSILON)
        + WEIGHT_DECAY * master[0].T
    )
    return gather_rows(update.astype(jnp.bfloat16).T, "dp")[None]


def solution(mesh):
    in_specs = (
        P("pipe", None, "dp", None),
        P("pipe", None, "dp", "tensor"),
        P("pipe", None),
        P("pipe", "dp", "tensor"),
        P("pipe", "dp", "tensor"),
        P("pipe", "dp", "tensor"),
    )
    out_specs = P("pipe", None, "tensor")
    return jax.shard_map(local, mesh=mesh, in_specs=in_specs, out_specs=out_specs, check_vma=False)
```

```python
import jax
import jax.numpy as jnp
from jax import lax
from jax.sharding import PartitionSpec as P

MOMENT_DECAY = 0.9
SQUARE_DECAY = 0.95
FIRST_CORRECTION = 1.0 - 0.9**20
SECOND_CORRECTION = 1.0 - 0.95**20
WEIGHT_DECAY = 0.1
CLIP_NORM = 1.0
EPSILON = 1e-08


def slot_term(inputs, key_grads, live_row, column_count):
    live = live_row[:, None, None] == 1
    weighted = jnp.where(live, key_grads, jnp.zeros_like(key_grads)).reshape(-1, key_grads.shape[2])
    columns = inputs.reshape(-1, column_count)
    return lax.dot_general(
        weighted, columns, (((0,), (0,)), ((), ())), preferred_element_type=jnp.float32
    )


def butterfly_sum(value, axes):
    for axis in axes:
        size = lax.axis_size(axis)
        if size & (size - 1):
            value = lax.psum(value, axis)
            continue
        bit = size // 2
        while bit >= 1:
            pairs = [(i, i ^ bit) for i in range(size)]
            value = value + lax.ppermute(value, axis, pairs)
            bit //= 2
    return value


def bit_orders(size):
    bits = list(range(size.bit_length() - 1))
    return bits, bits[1:2] + bits[:1] + bits[2:], bits[:1] + bits[2:3] + bits[1:2] + bits[3:]


def halving_scatter(partial, axis, order):
    size = lax.axis_size(axis)
    index = lax.axis_index(axis)
    width = partial.shape[1] // size
    held = list(range(size))
    blocks = partial
    for bit in order:
        mine = (index >> bit) & 1
        low = [k for k, block in enumerate(held) if not (block >> bit) & 1]
        high = [k for k, block in enumerate(held) if (block >> bit) & 1]
        low_part = jnp.concatenate([blocks[:, k * width:(k + 1) * width] for k in low], axis=1)
        high_part = jnp.concatenate([blocks[:, k * width:(k + 1) * width] for k in high], axis=1)
        keep = jnp.where(mine == 1, high_part, low_part)
        send = jnp.where(mine == 1, low_part, high_part)
        pairs = [(i, i ^ (1 << bit)) for i in range(size)]
        blocks = keep + lax.ppermute(send, axis, pairs)
        held = [held[k] & ~(1 << bit) for k in low]
    return blocks


def doubling_gather(part, axis, order):
    size = lax.axis_size(axis)
    levels = size.bit_length() - 1
    index = lax.axis_index(axis)
    placed = []
    current = part
    for bit in order:
        mine = (index >> bit) & 1
        pairs = [(i, i ^ (1 << bit)) for i in range(size)]
        other = lax.ppermute(current, axis, pairs)
        low = jnp.where(mine == 1, other, current)
        high = jnp.where(mine == 1, current, other)
        current = jnp.stack([low, high], axis=0)
        placed.insert(0, bit)
    perm = [placed.index(bit) for bit in range(levels - 1, -1, -1)]
    current = jnp.transpose(current, perm + list(range(levels, current.ndim)))
    return current.reshape((-1,) + part.shape[1:])


def scatter_rows(partial_t, axis, parts=4):
    size = lax.axis_size(axis)
    cols = partial_t.shape[0]
    if size & (size - 1) or size == 1 or cols % (8 * parts):
        return lax.psum_scatter(partial_t, axis, scatter_dimension=1, tiled=True)
    orders = bit_orders(size)
    width = cols // parts
    return jnp.concatenate(
        [
            halving_scatter(partial_t[k * width:(k + 1) * width], axis, orders[(1, 0, 1, 2)[k % 4]])
            for k in range(parts)
        ],
        axis=0,
    )


def gather_rows(part, axis):
    size = lax.axis_size(axis)
    cols = part.shape[1]
    if size & (size - 1) or size == 1 or cols % 2:
        return lax.all_gather(part, axis, axis=0, tiled=True)
    first, second = bit_orders(size)[:2]
    half = cols // 2
    return jnp.concatenate(
        [
            doubling_gather(part[:, :half], axis, first[::-1]),
            doubling_gather(part[:, half:], axis, bit_orders(size)[2]),
        ],
        axis=1,
    )


def local(normed_input, key_grad, live_slots, master, first_moment, second_moment):
    inputs = normed_input[0]
    key_grads = key_grad[0]
    live_row = live_slots[0]
    live_count = jnp.sum(live_row)
    features = inputs.shape[2]
    summed = scatter_rows(slot_term(inputs, key_grads, live_row, features), "dp")
    tokens_total = (live_count * (inputs.shape[1] * lax.axis_size("dp"))).astype(jnp.float32)
    grad_shard = summed / tokens_total
    squares = butterfly_sum(jnp.sum(grad_shard * grad_shard), ("tensor", "pipe", "dp"))
    clip_factor = jnp.minimum(1.0, CLIP_NORM / jnp.sqrt(squares))
    clipped = clip_factor * grad_shard
    moment1 = MOMENT_DECAY * first_moment[0].T + (1.0 - MOMENT_DECAY) * clipped
    moment2 = SQUARE_DECAY * second_moment[0].T + (1.0 - SQUARE_DECAY) * clipped * clipped
    update = (
        moment1 / FIRST_CORRECTION / (jnp.sqrt(moment2 / SECOND_CORRECTION) + EPSILON)
        + WEIGHT_DECAY * master[0].T
    )
    return gather_rows(update.astype(jnp.bfloat16).T, "dp")[None]


def solution(mesh):
    in_specs = (
        P("pipe", None, "dp", None),
        P("pipe", None, "dp", "tensor"),
        P("pipe", None),
        P("pipe", "dp", "tensor"),
        P("pipe", "dp", "tensor"),
        P("pipe", "dp", "tensor"),
    )
    out_specs = P("pipe", None, "tensor")
    return jax.shard_map(local, mesh=mesh, in_specs=in_specs, out_specs=out_specs, check_vma=False)
```

```python
import jax
import jax.numpy as jnp
from jax import lax
from jax.sharding import PartitionSpec as P

MOMENT_DECAY = 0.9
SQUARE_DECAY = 0.95
FIRST_CORRECTION = 1.0 - 0.9**20
SECOND_CORRECTION = 1.0 - 0.95**20
WEIGHT_DECAY = 0.1
CLIP_NORM = 1.0
EPSILON = 1e-08


def slot_term(inputs, key_grads, live_row, column_count):
    live = live_row[:, None, None] == 1
    weighted = jnp.where(live, key_grads, jnp.zeros_like(key_grads)).reshape(-1, key_grads.shape[2])
    columns = inputs.reshape(-1, column_count)
    return lax.dot_general(
        weighted, columns, (((0,), (0,)), ((), ())), preferred_element_type=jnp.float32
    )


def butterfly_sum(value, axes):
    for axis in axes:
        size = lax.axis_size(axis)
        if size & (size - 1):
            value = lax.psum(value, axis)
            continue
        bit = size // 2
        while bit >= 1:
            pairs = [(i, i ^ bit) for i in range(size)]
            value = value + lax.ppermute(value, axis, pairs)
            bit //= 2
    return value


def bit_orders(size):
    bits = list(range(size.bit_length() - 1))
    return bits, bits[1:2] + bits[:1] + bits[2:], bits[:1] + bits[2:3] + bits[1:2] + bits[3:]


def halving_scatter(partial, axis, order):
    size = lax.axis_size(axis)
    index = lax.axis_index(axis)
    width = partial.shape[1] // size
    held = list(range(size))
    blocks = partial
    for bit in order:
        mine = (index >> bit) & 1
        low = [k for k, block in enumerate(held) if not (block >> bit) & 1]
        high = [k for k, block in enumerate(held) if (block >> bit) & 1]
        low_part = jnp.concatenate([blocks[:, k * width:(k + 1) * width] for k in low], axis=1)
        high_part = jnp.concatenate([blocks[:, k * width:(k + 1) * width] for k in high], axis=1)
        keep = jnp.where(mine == 1, high_part, low_part)
        send = jnp.where(mine == 1, low_part, high_part)
        pairs = [(i, i ^ (1 << bit)) for i in range(size)]
        blocks = keep + lax.ppermute(send, axis, pairs)
        held = [held[k] & ~(1 << bit) for k in low]
    return blocks


def doubling_gather(part, axis, order):
    size = lax.axis_size(axis)
    levels = size.bit_length() - 1
    index = lax.axis_index(axis)
    placed = []
    current = part
    for bit in order:
        mine = (index >> bit) & 1
        pairs = [(i, i ^ (1 << bit)) for i in range(size)]
        other = lax.ppermute(current, axis, pairs)
        low = jnp.where(mine == 1, other, current)
        high = jnp.where(mine == 1, current, other)
        current = jnp.stack([low, high], axis=0)
        placed.insert(0, bit)
    perm = [placed.index(bit) for bit in range(levels - 1, -1, -1)]
    current = jnp.transpose(current, perm + list(range(levels, current.ndim)))
    return current.reshape((-1,) + part.shape[1:])


def scatter_rows(partial_t, axis, parts=4):
    size = lax.axis_size(axis)
    cols = partial_t.shape[0]
    if size & (size - 1) or size == 1 or cols % (8 * parts):
        return lax.psum_scatter(partial_t, axis, scatter_dimension=1, tiled=True)
    orders = bit_orders(size)
    width = cols // parts
    return jnp.concatenate(
        [
            halving_scatter(partial_t[k * width:(k + 1) * width], axis, orders[(0, 1, 2, 1)[k % 4]])
            for k in range(parts)
        ],
        axis=0,
    )


def gather_rows(part, axis):
    size = lax.axis_size(axis)
    cols = part.shape[1]
    if size & (size - 1) or size == 1 or cols % 2:
        return lax.all_gather(part, axis, axis=0, tiled=True)
    first, second = bit_orders(size)[:2]
    half = cols // 2
    return jnp.concatenate(
        [
            doubling_gather(part[:, :half], axis, bit_orders(size)[2]),
            doubling_gather(part[:, half:], axis, first[::-1]),
        ],
        axis=1,
    )


def local(normed_input, key_grad, live_slots, master, first_moment, second_moment):
    inputs = normed_input[0]
    key_grads = key_grad[0]
    live_row = live_slots[0]
    live_count = jnp.sum(live_row)
    features = inputs.shape[2]
    summed = scatter_rows(slot_term(inputs, key_grads, live_row, features), "dp")
    tokens_total = (live_count * (inputs.shape[1] * lax.axis_size("dp"))).astype(jnp.float32)
    grad_shard = summed / tokens_total
    squares = butterfly_sum(jnp.sum(grad_shard * grad_shard), ("tensor", "pipe", "dp"))
    clip_factor = jnp.minimum(1.0, CLIP_NORM / jnp.sqrt(squares))
    clipped = clip_factor * grad_shard
    moment1 = MOMENT_DECAY * first_moment[0].T + (1.0 - MOMENT_DECAY) * clipped
    moment2 = SQUARE_DECAY * second_moment[0].T + (1.0 - SQUARE_DECAY) * clipped * clipped
    update = (
        moment1 / FIRST_CORRECTION / (jnp.sqrt(moment2 / SECOND_CORRECTION) + EPSILON)
        + WEIGHT_DECAY * master[0].T
    )
    return gather_rows(update.astype(jnp.bfloat16).T, "dp")[None]


def solution(mesh):
    in_specs = (
        P("pipe", None, "dp", None),
        P("pipe", None, "dp", "tensor"),
        P("pipe", None),
        P("pipe", "dp", "tensor"),
        P("pipe", "dp", "tensor"),
        P("pipe", "dp", "tensor"),
    )
    out_specs = P("pipe", None, "tensor")
    return jax.shard_map(local, mesh=mesh, in_specs=in_specs, out_specs=out_specs, check_vma=False)
```

```python
import jax
import jax.numpy as jnp
from jax import lax
from jax.sharding import PartitionSpec as P

MOMENT_DECAY = 0.9
SQUARE_DECAY = 0.95
FIRST_CORRECTION = 1.0 - 0.9**20
SECOND_CORRECTION = 1.0 - 0.95**20
WEIGHT_DECAY = 0.1
CLIP_NORM = 1.0
EPSILON = 1e-08


def slot_term(inputs, key_grads, live_row, column_count):
    live = live_row[:, None, None] == 1
    weighted = jnp.where(live, key_grads, jnp.zeros_like(key_grads)).reshape(-1, key_grads.shape[2])
    columns = inputs.reshape(-1, column_count)
    return lax.dot_general(
        weighted, columns, (((0,), (0,)), ((), ())), preferred_element_type=jnp.float32
    )


def butterfly_sum(value, axes):
    for axis in axes:
        size = lax.axis_size(axis)
        if size & (size - 1):
            value = lax.psum(value, axis)
            continue
        bit = size // 2
        while bit >= 1:
            pairs = [(i, i ^ bit) for i in range(size)]
            value = value + lax.ppermute(value, axis, pairs)
            bit //= 2
    return value


def bit_orders(size):
    bits = list(range(size.bit_length() - 1))
    return bits, bits[1:2] + bits[:1] + bits[2:], bits[:1] + bits[2:3] + bits[1:2] + bits[3:]


def halving_scatter(partial, axis, order):
    size = lax.axis_size(axis)
    index = lax.axis_index(axis)
    width = partial.shape[1] // size
    held = list(range(size))
    blocks = partial
    for bit in order:
        mine = (index >> bit) & 1
        low = [k for k, block in enumerate(held) if not (block >> bit) & 1]
        high = [k for k, block in enumerate(held) if (block >> bit) & 1]
        low_part = jnp.concatenate([blocks[:, k * width:(k + 1) * width] for k in low], axis=1)
        high_part = jnp.concatenate([blocks[:, k * width:(k + 1) * width] for k in high], axis=1)
        keep = jnp.where(mine == 1, high_part, low_part)
        send = jnp.where(mine == 1, low_part, high_part)
        pairs = [(i, i ^ (1 << bit)) for i in range(size)]
        blocks = keep + lax.ppermute(send, axis, pairs)
        held = [held[k] & ~(1 << bit) for k in low]
    return blocks


def doubling_gather(part, axis, order):
    size = lax.axis_size(axis)
    levels = size.bit_length() - 1
    index = lax.axis_index(axis)
    placed = []
    current = part
    for bit in order:
        mine = (index >> bit) & 1
        pairs = [(i, i ^ (1 << bit)) for i in range(size)]
        other = lax.ppermute(current, axis, pairs)
        low = jnp.where(mine == 1, other, current)
        high = jnp.where(mine == 1, current, other)
        current = jnp.stack([low, high], axis=0)
        placed.insert(0, bit)
    perm = [placed.index(bit) for bit in range(levels - 1, -1, -1)]
    current = jnp.transpose(current, perm + list(range(levels, current.ndim)))
    return current.reshape((-1,) + part.shape[1:])


def scatter_rows(partial_t, axis, parts=4):
    size = lax.axis_size(axis)
    cols = partial_t.shape[0]
    if size & (size - 1) or size == 1 or cols % (8 * parts):
        return lax.psum_scatter(partial_t, axis, scatter_dimension=1, tiled=True)
    orders = bit_orders(size)
    width = cols // parts
    return jnp.concatenate(
        [
            halving_scatter(partial_t[k * width:(k + 1) * width], axis, orders[(0, 1, 2, 1)[k % 4]])
            for k in range(parts)
        ],
        axis=0,
    )


def gather_rows(part, axis):
    size = lax.axis_size(axis)
    cols = part.shape[1]
    if size & (size - 1) or size == 1 or cols % 2:
        return lax.all_gather(part, axis, axis=0, tiled=True)
    first, second = bit_orders(size)[:2]
    half = cols // 2
    return jnp.concatenate(
        [
            doubling_gather(part[:, :half], axis, first[::-1]),
            doubling_gather(part[:, half:], axis, bit_orders(size)[2]),
        ],
        axis=1,
    )


def local(normed_input, key_grad, live_slots, master, first_moment, second_moment):
    inputs = normed_input[0]
    key_grads = key_grad[0]
    live_row = live_slots[0]
    live_count = jnp.sum(live_row)
    features = inputs.shape[2]
    summed = scatter_rows(slot_term(inputs, key_grads, live_row, features), "dp")
    tokens_total = (live_count * (inputs.shape[1] * lax.axis_size("dp"))).astype(jnp.float32)
    grad_shard = summed / tokens_total
    squares = butterfly_sum(jnp.sum(grad_shard * grad_shard), ("pipe", "dp", "tensor"))
    clip_factor = jnp.minimum(1.0, CLIP_NORM / jnp.sqrt(squares))
    clipped = clip_factor * grad_shard
    moment1 = MOMENT_DECAY * first_moment[0].T + (1.0 - MOMENT_DECAY) * clipped
    moment2 = SQUARE_DECAY * second_moment[0].T + (1.0 - SQUARE_DECAY) * clipped * clipped
    update = (
        moment1 / FIRST_CORRECTION / (jnp.sqrt(moment2 / SECOND_CORRECTION) + EPSILON)
        + WEIGHT_DECAY * master[0].T
    )
    return gather_rows(update.astype(jnp.bfloat16).T, "dp")[None]


def solution(mesh):
    in_specs = (
        P("pipe", None, "dp", None),
        P("pipe", None, "dp", "tensor"),
        P("pipe", None),
        P("pipe", "dp", "tensor"),
        P("pipe", "dp", "tensor"),
        P("pipe", "dp", "tensor"),
    )
    out_specs = P("pipe", None, "tensor")
    return jax.shard_map(local, mesh=mesh, in_specs=in_specs, out_specs=out_specs, check_vma=False)
```

```python
import jax
import jax.numpy as jnp
from jax import lax
from jax.sharding import PartitionSpec as P

MOMENT_DECAY = 0.9
SQUARE_DECAY = 0.95
FIRST_CORRECTION = 1.0 - 0.9**20
SECOND_CORRECTION = 1.0 - 0.95**20
WEIGHT_DECAY = 0.1
CLIP_NORM = 1.0
EPSILON = 1e-08


def slot_term(inputs, key_grads, live_row, column_count):
    live = live_row[:, None, None] == 1
    weighted = jnp.where(live, key_grads, jnp.zeros_like(key_grads)).reshape(-1, key_grads.shape[2])
    columns = inputs.reshape(-1, column_count)
    return lax.dot_general(
        weighted, columns, (((0,), (0,)), ((), ())), preferred_element_type=jnp.float32
    )


def butterfly_sum(value, axes):
    for axis in axes:
        size = lax.axis_size(axis)
        if size & (size - 1):
            value = lax.psum(value, axis)
            continue
        bit = size // 2
        while bit >= 1:
            pairs = [(i, i ^ bit) for i in range(size)]
            value = value + lax.ppermute(value, axis, pairs)
            bit //= 2
    return value


def bit_orders(size):
    bits = list(range(size.bit_length() - 1))
    return bits, bits[1:2] + bits[:1] + bits[2:], bits[:1] + bits[2:3] + bits[1:2] + bits[3:]


def halving_scatter(partial, axis, order):
    size = lax.axis_size(axis)
    index = lax.axis_index(axis)
    width = partial.shape[1] // size
    held = list(range(size))
    blocks = partial
    for bit in order:
        mine = (index >> bit) & 1
        low = [k for k, block in enumerate(held) if not (block >> bit) & 1]
        high = [k for k, block in enumerate(held) if (block >> bit) & 1]
        low_part = jnp.concatenate([blocks[:, k * width:(k + 1) * width] for k in low], axis=1)
        high_part = jnp.concatenate([blocks[:, k * width:(k + 1) * width] for k in high], axis=1)
        keep = jnp.where(mine == 1, high_part, low_part)
        send = jnp.where(mine == 1, low_part, high_part)
        pairs = [(i, i ^ (1 << bit)) for i in range(size)]
        blocks = keep + lax.ppermute(send, axis, pairs)
        held = [held[k] & ~(1 << bit) for k in low]
    return blocks


def doubling_gather(part, axis, order):
    size = lax.axis_size(axis)
    levels = size.bit_length() - 1
    index = lax.axis_index(axis)
    placed = []
    current = part
    for bit in order:
        mine = (index >> bit) & 1
        pairs = [(i, i ^ (1 << bit)) for i in range(size)]
        other = lax.ppermute(current, axis, pairs)
        low = jnp.where(mine == 1, other, current)
        high = jnp.where(mine == 1, current, other)
        current = jnp.stack([low, high], axis=0)
        placed.insert(0, bit)
    perm = [placed.index(bit) for bit in range(levels - 1, -1, -1)]
    current = jnp.transpose(current, perm + list(range(levels, current.ndim)))
    return current.reshape((-1,) + part.shape[1:])


def scatter_rows(partial_t, axis, parts=4):
    size = lax.axis_size(axis)
    cols = partial_t.shape[0]
    if size & (size - 1) or size == 1 or cols % (8 * parts):
        return lax.psum_scatter(partial_t, axis, scatter_dimension=1, tiled=True)
    orders = bit_orders(size)
    width = cols // parts
    return jnp.concatenate(
        [
            halving_scatter(partial_t[k * width:(k + 1) * width], axis, orders[(2, 1, 0, 1)[k % 4]])
            for k in range(parts)
        ],
        axis=0,
    )


def gather_rows(part, axis):
    size = lax.axis_size(axis)
    cols = part.shape[1]
    if size & (size - 1) or size == 1 or cols % 2:
        return lax.all_gather(part, axis, axis=0, tiled=True)
    first, second = bit_orders(size)[:2]
    half = cols // 2
    return jnp.concatenate(
        [
            doubling_gather(part[:, :half], axis, first[::-1]),
            doubling_gather(part[:, half:], axis, bit_orders(size)[2]),
        ],
        axis=1,
    )


def local(normed_input, key_grad, live_slots, master, first_moment, second_moment):
    inputs = normed_input[0]
    key_grads = key_grad[0]
    live_row = live_slots[0]
    live_count = jnp.sum(live_row)
    features = inputs.shape[2]
    summed = scatter_rows(slot_term(inputs, key_grads, live_row, features), "dp")
    tokens_total = (live_count * (inputs.shape[1] * lax.axis_size("dp"))).astype(jnp.float32)
    grad_shard = summed / tokens_total
    squares = butterfly_sum(jnp.sum(grad_shard * grad_shard), ("tensor", "pipe", "dp"))
    clip_factor = jnp.minimum(1.0, CLIP_NORM / jnp.sqrt(squares))
    clipped = clip_factor * grad_shard
    moment1 = MOMENT_DECAY * first_moment[0].T + (1.0 - MOMENT_DECAY) * clipped
    moment2 = SQUARE_DECAY * second_moment[0].T + (1.0 - SQUARE_DECAY) * clipped * clipped
    update = (
        moment1 / FIRST_CORRECTION / (jnp.sqrt(moment2 / SECOND_CORRECTION) + EPSILON)
        + WEIGHT_DECAY * master[0].T
    )
    return gather_rows(update.astype(jnp.bfloat16).T, "dp")[None]


def solution(mesh):
    in_specs = (
        P("pipe", None, "dp", None),
        P("pipe", None, "dp", "tensor"),
        P("pipe", None),
        P("pipe", "dp", "tensor"),
        P("pipe", "dp", "tensor"),
        P("pipe", "dp", "tensor"),
    )
    out_specs = P("pipe", None, "tensor")
    return jax.shard_map(local, mesh=mesh, in_specs=in_specs, out_specs=out_specs, check_vma=False)
```

```python
import jax
import jax.numpy as jnp
from jax import lax
from jax.sharding import PartitionSpec as P

MOMENT_DECAY = 0.9
SQUARE_DECAY = 0.95
FIRST_CORRECTION = 1.0 - 0.9**20
SECOND_CORRECTION = 1.0 - 0.95**20
WEIGHT_DECAY = 0.1
CLIP_NORM = 1.0
EPSILON = 1e-08


def slot_term(inputs, key_grads, live_row, column_count):
    live = live_row[:, None, None] == 1
    weighted = jnp.where(live, key_grads, jnp.zeros_like(key_grads)).reshape(-1, key_grads.shape[2])
    columns = inputs.reshape(-1, column_count)
    return lax.dot_general(
        weighted, columns, (((0,), (0,)), ((), ())), preferred_element_type=jnp.float32
    )


def butterfly_sum(value, axes):
    for axis in axes:
        size = lax.axis_size(axis)
        if size & (size - 1):
            value = lax.psum(value, axis)
            continue
        bit = size // 2
        while bit >= 1:
            pairs = [(i, i ^ bit) for i in range(size)]
            value = value + lax.ppermute(value, axis, pairs)
            bit //= 2
    return value


def bit_orders(size):
    bits = list(range(size.bit_length() - 1))
    return bits, bits[1:2] + bits[:1] + bits[2:], bits[:1] + bits[2:3] + bits[1:2] + bits[3:]


def halving_scatter(partial, axis, order):
    size = lax.axis_size(axis)
    index = lax.axis_index(axis)
    width = partial.shape[1] // size
    held = list(range(size))
    blocks = partial
    for bit in order:
        mine = (index >> bit) & 1
        low = [k for k, block in enumerate(held) if not (block >> bit) & 1]
        high = [k for k, block in enumerate(held) if (block >> bit) & 1]
        low_part = jnp.concatenate([blocks[:, k * width:(k + 1) * width] for k in low], axis=1)
        high_part = jnp.concatenate([blocks[:, k * width:(k + 1) * width] for k in high], axis=1)
        keep = jnp.where(mine == 1, high_part, low_part)
        send = jnp.where(mine == 1, low_part, high_part)
        pairs = [(i, i ^ (1 << bit)) for i in range(size)]
        blocks = keep + lax.ppermute(send, axis, pairs)
        held = [held[k] & ~(1 << bit) for k in low]
    return blocks


def doubling_gather(part, axis, order):
    size = lax.axis_size(axis)
    levels = size.bit_length() - 1
    index = lax.axis_index(axis)
    placed = []
    current = part
    for bit in order:
        mine = (index >> bit) & 1
        pairs = [(i, i ^ (1 << bit)) for i in range(size)]
        other = lax.ppermute(current, axis, pairs)
        low = jnp.where(mine == 1, other, current)
        high = jnp.where(mine == 1, current, other)
        current = jnp.stack([low, high], axis=0)
        placed.insert(0, bit)
    perm = [placed.index(bit) for bit in range(levels - 1, -1, -1)]
    current = jnp.transpose(current, perm + list(range(levels, current.ndim)))
    return current.reshape((-1,) + part.shape[1:])


def scatter_rows(partial_t, axis, parts=4):
    size = lax.axis_size(axis)
    cols = partial_t.shape[0]
    if size & (size - 1) or size == 1 or cols % (8 * parts):
        return lax.psum_scatter(partial_t, axis, scatter_dimension=1, tiled=True)
    orders = bit_orders(size)
    width = cols // parts
    return jnp.concatenate(
        [
            halving_scatter(partial_t[k * width:(k + 1) * width], axis, orders[(2, 0, 1, 1)[k % 4]])
            for k in range(parts)
        ],
        axis=0,
    )


def gather_rows(part, axis):
    size = lax.axis_size(axis)
    cols = part.shape[1]
    if size & (size - 1) or size == 1 or cols % 2:
        return lax.all_gather(part, axis, axis=0, tiled=True)
    first, second = bit_orders(size)[:2]
    half = cols // 2
    return jnp.concatenate(
        [
            doubling_gather(part[:, :half], axis, first[::-1]),
            doubling_gather(part[:, half:], axis, bit_orders(size)[2]),
        ],
        axis=1,
    )


def local(normed_input, key_grad, live_slots, master, first_moment, second_moment):
    inputs = normed_input[0]
    key_grads = key_grad[0]
    live_row = live_slots[0]
    live_count = jnp.sum(live_row)
    features = inputs.shape[2]
    summed = scatter_rows(slot_term(inputs, key_grads, live_row, features), "dp")
    tokens_total = (live_count * (inputs.shape[1] * lax.axis_size("dp"))).astype(jnp.float32)
    grad_shard = summed / tokens_total
    squares = butterfly_sum(jnp.sum(grad_shard * grad_shard), ("tensor", "pipe", "dp"))
    clip_factor = jnp.minimum(1.0, CLIP_NORM / jnp.sqrt(squares))
    clipped = clip_factor * grad_shard
    moment1 = MOMENT_DECAY * first_moment[0].T + (1.0 - MOMENT_DECAY) * clipped
    moment2 = SQUARE_DECAY * second_moment[0].T + (1.0 - SQUARE_DECAY) * clipped * clipped
    update = (
        moment1 / FIRST_CORRECTION / (jnp.sqrt(moment2 / SECOND_CORRECTION) + EPSILON)
        + WEIGHT_DECAY * master[0].T
    )
    return gather_rows(update.astype(jnp.bfloat16).T, "dp")[None]


def solution(mesh):
    in_specs = (
        P("pipe", None, "dp", None),
        P("pipe", None, "dp", "tensor"),
        P("pipe", None),
        P("pipe", "dp", "tensor"),
        P("pipe", "dp", "tensor"),
        P("pipe", "dp", "tensor"),
    )
    out_specs = P("pipe", None, "tensor")
    return jax.shard_map(local, mesh=mesh, in_specs=in_specs, out_specs=out_specs, check_vma=False)
```

```python
import jax
import jax.numpy as jnp
from jax import lax
from jax.sharding import PartitionSpec as P

MOMENT_DECAY = 0.9
SQUARE_DECAY = 0.95
FIRST_CORRECTION = 1.0 - 0.9**20
SECOND_CORRECTION = 1.0 - 0.95**20
WEIGHT_DECAY = 0.1
CLIP_NORM = 1.0
EPSILON = 1e-08


def slot_term(inputs, key_grads, live_row, column_count):
    live = live_row[:, None, None] == 1
    weighted = jnp.where(live, key_grads, jnp.zeros_like(key_grads)).reshape(-1, key_grads.shape[2])
    columns = inputs.reshape(-1, column_count)
    return lax.dot_general(
        weighted, columns, (((0,), (0,)), ((), ())), preferred_element_type=jnp.float32
    )


def butterfly_sum(value, axes):
    for axis in axes:
        size = lax.axis_size(axis)
        if size & (size - 1):
            value = lax.psum(value, axis)
            continue
        bit = size // 2
        while bit >= 1:
            pairs = [(i, i ^ bit) for i in range(size)]
            value = value + lax.ppermute(value, axis, pairs)
            bit //= 2
    return value


def bit_orders(size):
    bits = list(range(size.bit_length() - 1))
    return bits, bits[1:2] + bits[:1] + bits[2:], bits[:1] + bits[2:3] + bits[1:2] + bits[3:]


def halving_scatter(partial, axis, order):
    size = lax.axis_size(axis)
    index = lax.axis_index(axis)
    width = partial.shape[1] // size
    held = list(range(size))
    blocks = partial
    for bit in order:
        mine = (index >> bit) & 1
        low = [k for k, block in enumerate(held) if not (block >> bit) & 1]
        high = [k for k, block in enumerate(held) if (block >> bit) & 1]
        low_part = jnp.concatenate([blocks[:, k * width:(k + 1) * width] for k in low], axis=1)
        high_part = jnp.concatenate([blocks[:, k * width:(k + 1) * width] for k in high], axis=1)
        keep = jnp.where(mine == 1, high_part, low_part)
        send = jnp.where(mine == 1, low_part, high_part)
        pairs = [(i, i ^ (1 << bit)) for i in range(size)]
        blocks = keep + lax.ppermute(send, axis, pairs)
        held = [held[k] & ~(1 << bit) for k in low]
    return blocks


def doubling_gather(part, axis, order):
    size = lax.axis_size(axis)
    levels = size.bit_length() - 1
    index = lax.axis_index(axis)
    placed = []
    current = part
    for bit in order:
        mine = (index >> bit) & 1
        pairs = [(i, i ^ (1 << bit)) for i in range(size)]
        other = lax.ppermute(current, axis, pairs)
        low = jnp.where(mine == 1, other, current)
        high = jnp.where(mine == 1, current, other)
        current = jnp.stack([low, high], axis=0)
        placed.insert(0, bit)
    perm = [placed.index(bit) for bit in range(levels - 1, -1, -1)]
    current = jnp.transpose(current, perm + list(range(levels, current.ndim)))
    return current.reshape((-1,) + part.shape[1:])


def scatter_rows(partial_t, axis, parts=4):
    size = lax.axis_size(axis)
    cols = partial_t.shape[0]
    if size & (size - 1) or size == 1 or cols % (8 * parts):
        return lax.psum_scatter(partial_t, axis, scatter_dimension=1, tiled=True)
    orders = bit_orders(size)
    width = cols // parts
    return jnp.concatenate(
        [
            halving_scatter(partial_t[k * width:(k + 1) * width], axis, orders[(2, 1, 1, 0)[k % 4]])
            for k in range(parts)
        ],
        axis=0,
    )


def gather_rows(part, axis):
    size = lax.axis_size(axis)
    cols = part.shape[1]
    if size & (size - 1) or size == 1 or cols % 2:
        return lax.all_gather(part, axis, axis=0, tiled=True)
    first, second = bit_orders(size)[:2]
    half = cols // 2
    return jnp.concatenate(
        [
            doubling_gather(part[:, :half], axis, first[::-1]),
            doubling_gather(part[:, half:], axis, bit_orders(size)[2]),
        ],
        axis=1,
    )


def local(normed_input, key_grad, live_slots, master, first_moment, second_moment):
    inputs = normed_input[0]
    key_grads = key_grad[0]
    live_row = live_slots[0]
    live_count = jnp.sum(live_row)
    features = inputs.shape[2]
    summed = scatter_rows(slot_term(inputs, key_grads, live_row, features), "dp")
    tokens_total = (live_count * (inputs.shape[1] * lax.axis_size("dp"))).astype(jnp.float32)
    grad_shard = summed / tokens_total
    squares = butterfly_sum(jnp.sum(grad_shard * grad_shard), ("tensor", "pipe", "dp"))
    clip_factor = jnp.minimum(1.0, CLIP_NORM / jnp.sqrt(squares))
    clipped = clip_factor * grad_shard
    moment1 = MOMENT_DECAY * first_moment[0].T + (1.0 - MOMENT_DECAY) * clipped
    moment2 = SQUARE_DECAY * second_moment[0].T + (1.0 - SQUARE_DECAY) * clipped * clipped
    update = (
        moment1 / FIRST_CORRECTION / (jnp.sqrt(moment2 / SECOND_CORRECTION) + EPSILON)
        + WEIGHT_DECAY * master[0].T
    )
    return gather_rows(update.astype(jnp.bfloat16).T, "dp")[None]


def solution(mesh):
    in_specs = (
        P("pipe", None, "dp", None),
        P("pipe", None, "dp", "tensor"),
        P("pipe", None),
        P("pipe", "dp", "tensor"),
        P("pipe", "dp", "tensor"),
        P("pipe", "dp", "tensor"),
    )
    out_specs = P("pipe", None, "tensor")
    return jax.shard_map(local, mesh=mesh, in_specs=in_specs, out_specs=out_specs, check_vma=False)
```
